32 devices in a mesh: region: 4 (over z), sub: 8 (over y, x, core).
Axes of the slice: x: 2, y: 2, z: 4, core: 2. Of those that a mesh axis runs over, the one named last changes fastest.
Arguments:
- feats: bfloat16 [16384, 1536], P(('region', 'sub')), may hold values from -6 to 6
- conv_weight: bfloat16 [192, 128], replicated, may hold values from -0.4375 to 0.4375
- conv_bias: float32 [128], replicated, may hold values from -3 to 3
- theta: bfloat16 [64, 64], replicated, may hold values from -0.75 to 0.75
- edge_weight: float32 [4096], P(('region', 'sub')), may hold values from 1 to 4
- inner_edge: int32 [16384, 2], P(('region', 'sub')), may hold values from 0 to 127
- crossing_segment: int32 [4096], P(('region', 'sub')), may hold values from 0 to 511
- cut_dest: int32 [4096, 1], P(('region', 'sub')), may hold values from 0 to 31; in each aligned block of 128 rows (0 to 127, 128 to 255, ...) at most 8 rows name the same one
- crossing_hyperedge: int32 [4096], P(('region', 'sub')), may hold values from 0 to 127
- cotangent: bfloat16 [16384, 1280], P(('region', 'sub')), may hold values from -6 to 6
Outputs:
- block_out: bfloat16 [16384, 1280], P(('region', 'sub'))
- grad_feats: bfloat16 [16384, 1536], P(('region', 'sub'))
- grad_conv: float32 [192, 128], replicated
- grad_bias: float32 [128], replicated
- grad_theta: float32 [64, 64], replicated
The draws below stay inside these ranges and needn't reach their ends.
Inputs may be any that keep to these rules, and one draw needn't show every extreme that they name: `cut_dest`: among the 128 cut memberships of one device no owner is named more than 8 times; in some device one owner is named exactly 8 times.
All inputs are finite; a program needn't handle non-finite values.
Results may differ from the reference program's by a relative error of at most 0.0072.
Values may be sent and summed in bfloat16 or wider, within the bound.
No kernel may reach another device: no remote copies, remote signals or barrier semaphores. Data moves between devices by JAX's collectives and lax.ppermute only.
A program may use at most 64 MiB of HBM per device.

```python
import math
import jax
import jax.numpy as jnp
import numpy as np
from jax import lax

C = 64
T_SIZE = 12
B = 2
KT = 3
MEM = 2
SEG_DEV = 512
TP = 10
NDEV = 32
EDGE_DEV = 128
CUT_DEV = 128
CAP = 8
NSEG = 16384
NEDGE = 4096
NCUT = 4096


def place_ends(drawn, stream_key, low, largest):
    longest = drawn.shape.index(max(drawn.shape))
    spots = []
    for shift in (0, 1):
        where = [jax.random.randint(jax.random.fold_in(stream_key, axis), (), 0, length) for axis, length in enumerate(drawn.shape)]
        where[longest] = (where[longest] + shift) % drawn.shape[longest]
        spots.append(tuple(where))
    return drawn.at[spots[0]].set(low).at[spots[1]].set(largest)


def block_scale(key, shape, pieces, low, top_value):
    loudness = 1.0
    for dim, blocks in pieces:
        draws = jax.random.uniform(jax.random.fold_in(jax.random.fold_in(key, 6), dim), (blocks,), jnp.float32, low / len(pieces), top_value / len(pieces))
        loudness = loudness * jnp.repeat(jnp.exp(draws), shape[dim] // blocks).reshape((-1,) + (1,) * (len(shape) - 1 - dim))
    return loudness


def shared_out(own_key, own, number, rows, count, top, limit, skew):
    sequence = jax.random.permutation(own_key, count)
    heavy_load, common = portions_of(count, rows * top, limit, skew, True), portions_of(count, rows * top, limit, skew, False)
    places = jnp.arange(count)

    def named(tallies, turn):
        used = int((tallies > 0).sum())
        fixed = max(1, used // 4)
        passed = fixed + (places - fixed + turn * (used - fixed)) % max(1, count - fixed)
        return jnp.zeros((count,), jnp.int32).at[sequence[jnp.where(places < fixed, places, passed)]].set(jnp.asarray(tallies, jnp.int32))

    tallies = jnp.where(number % 4 == 0, named(heavy_load, number // 4), named(common, number - number // 4 - 1))
    mixed = jax.random.permutation(jax.random.fold_in(own, 3), count)
    donor, sink = mixed[0:count // 2 * 2:2], mixed[1:count // 2 * 2:2]
    margin = jnp.minimum(tallies[donor] - 1, limit - tallies[sink]) // 2
    margin = jnp.where((donor == sequence[0]) | (sink == sequence[0]) | (tallies[sink] == 0), 0, jnp.maximum(margin, 0))
    passed = jax.random.randint(jax.random.fold_in(own, 4), (count // 2,), 0, 1 << 20) % (margin + 1)
    tallies = tallies.at[donor].add(-passed).at[sink].add(passed)
    items = jnp.searchsorted(jnp.cumsum(tallies), jnp.arange(rows * top), side="right").astype(jnp.int32)
    listing = items.reshape(top, rows).T
    listing = listing[jax.random.permutation(jax.random.fold_in(own, 1), rows)]
    turn = jax.random.randint(jax.random.fold_in(own, 2), (rows, 1), 0, top)
    return jnp.take_along_axis(listing, (jnp.arange(top)[None, :] + turn) % top, axis=1)


def portions_of(number_of, total, bound, lean, full):
    loads = [(1 << 20) // math.isqrt(grade ** lean) + 1 for grade in range(1, number_of + 1)]
    largest = bound if full else min(bound, max(-(-total // number_of), total * loads[0] // sum(loads)))
    least = 1 if total - largest >= number_of - 1 else 0
    counts, spare = [largest] + [least] * (number_of - 1), total - largest - least * (number_of - 1)
    while spare > 0:
        candidates = [i for i in range(1, number_of) if counts[i] < largest] or [i for i in range(1, number_of) if counts[i] < bound]
        whole, budget = sum([loads[i] for i in candidates]), spare
        for i in candidates:
            extra = min(bound - counts[i], max(1, budget * loads[i] // whole), spare)
            counts[i] = counts[i] + extra
            spare = spare - extra
    return np.array(counts)


def noise(key, dims, deviation, most, split=(), held_as=jnp.bfloat16):
    array = deviation * jax.random.normal(key, dims, jnp.float32)
    if split:
        array = array * block_scale(key, dims, split, -0.22, 0.18)
    return jnp.clip(array, -most, most).astype(held_as)


def setup_inputs(seed: int = 0) -> dict:
    splits = jax.random.split(jax.random.key(seed), 11)
    feats = noise(splits[0], (NSEG, T_SIZE * B * C), 1.0, 6.0, ((0, 32),))
    conv_weight = noise(splits[1], (KT * C, 2 * C), (KT * C) ** -0.5, 0.4375)
    conv_bias = noise(splits[2], (2 * C,), 0.5, 3.0, (), jnp.float32)
    theta = noise(splits[3], (C, C), C ** -0.5, 0.75)
    edge_weight = jnp.clip(jnp.exp(math.log(4.0) - 1.3862944 * jax.random.uniform(splits[4], (NEDGE,), jnp.float32) ** block_scale(splits[4], (NEDGE,), ((0, 32),), -0.2, 0.2)), 1.0, 4.0)
    inner_edge = place_ends(jax.random.randint(splits[5], (NSEG, MEM), 0, EDGE_DEV), jax.random.fold_in(splits[5], 1), 0, EDGE_DEV - 1).astype(jnp.int32)
    crossing_segment = place_ends(jax.random.randint(splits[6], (NCUT,), 0, SEG_DEV), jax.random.fold_in(splits[6], 1), 0, SEG_DEV - 1).astype(jnp.int32)
    cut_dest_keys = jax.random.split(jax.random.fold_in(splits[7], 1), NCUT // CUT_DEV)
    cut_dest_turns = jax.random.permutation(jax.random.fold_in(splits[7], 3), NCUT // CUT_DEV)
    cut_dest = jax.vmap(lambda own, number: shared_out(jax.random.fold_in(splits[7], 2), own, number, CUT_DEV, NDEV, 1, CAP, 2))(cut_dest_keys, cut_dest_turns).reshape((NCUT, 1))
    crossing_hyperedge = place_ends(jax.random.randint(splits[8], (NCUT,), 0, EDGE_DEV), jax.random.fold_in(splits[8], 1), 0, EDGE_DEV - 1).astype(jnp.int32)
    cotangent = noise(splits[9], (NSEG, TP * B * C), 1.0, 6.0, ((0, 32),))
    return dict(feats=feats, conv_weight=conv_weight, conv_bias=conv_bias, theta=theta, edge_weight=edge_weight, inner_edge=inner_edge, crossing_segment=crossing_segment, cut_dest=cut_dest, crossing_hyperedge=crossing_hyperedge, cotangent=cotangent)


def conv_front(xb, conv_weight, conv_bias):
    x4 = xb.reshape(-1, T_SIZE, B, C).astype(jnp.float32)
    stack = jnp.concatenate([x4[:, k:k + TP] for k in range(KT)], axis=-1)
    u = jnp.einsum('stbk,kf->stbf', stack, conv_weight.astype(jnp.float32)) + conv_bias
    return (stack, u)

def forward_block(xb, conv_weight, conv_bias, theta):
    stack, u = conv_front(xb, conv_weight, conv_bias)
    gate = jax.nn.sigmoid(u[..., C:])
    hidden = (u[..., :C] * gate).astype(jnp.bfloat16)
    z = jnp.einsum('stbc,cd->stbd', hidden.astype(jnp.float32), theta.astype(jnp.float32)).astype(jnp.bfloat16)
    return z.reshape(xb.shape[0], -1)

def backward_block(xb, dzb, conv_weight, conv_bias, theta):
    stack, u = conv_front(xb, conv_weight, conv_bias)
    gate = jax.nn.sigmoid(u[..., C:])
    first = u[..., :C]
    hidden = (first * gate).astype(jnp.bfloat16).astype(jnp.float32)
    dz = dzb.reshape(-1, TP, B, C).astype(jnp.float32)
    g_theta = jnp.einsum('stbc,stbd->cd', hidden, dz)
    dh = jnp.einsum('stbd,cd->stbc', dz, theta.astype(jnp.float32))
    du = jnp.concatenate([dh * gate, dh * first * gate * (1.0 - gate)], axis=-1).astype(jnp.bfloat16).astype(jnp.float32)
    g_conv = jnp.einsum('stbk,stbf->kf', stack, du)
    g_bias = lax.optimization_barrier(jnp.sum(du, axis=(0, 1, 2)))
    dstack = jnp.einsum('stbf,kf->stbk', du, conv_weight.astype(jnp.float32))
    dx = jnp.zeros((xb.shape[0], T_SIZE, B, C), jnp.float32)
    for k in range(KT):
        dx = dx + jnp.pad(dstack[..., k * C:(k + 1) * C], ((0, 0), (k, KT - 1 - k), (0, 0), (0, 0)))
    return (dx.astype(jnp.bfloat16).reshape(xb.shape[0], -1), g_conv, g_bias, g_theta)

def reference(feats, conv_weight, conv_bias, theta, edge_weight, inner_edge, crossing_segment, cut_dest, crossing_hyperedge, cotangent):
    nseg = feats.shape[0]
    nblk = nseg // SEG_DEV
    nedge = EDGE_DEV * nblk
    xs = feats.reshape(nblk, SEG_DEV, -1)
    z = lax.map(lambda xb: forward_block(xb, conv_weight, conv_bias, theta), xs).reshape(nseg, -1)
    zf = z.astype(jnp.float32)
    rows = jnp.arange(nseg, dtype=jnp.int32)
    inner_g = (rows // SEG_DEV)[:, None] * EDGE_DEV + inner_edge
    ncut = crossing_segment.shape[0]
    cut_dev = jnp.arange(ncut, dtype=jnp.int32) // CUT_DEV
    cut_row = cut_dev * SEG_DEV + crossing_segment
    cut_g = cut_dest[:, 0] * EDGE_DEV + crossing_hyperedge
    ones_seg = jnp.ones((nseg,), jnp.float32)
    ones_cut = jnp.ones((ncut,), jnp.float32)
    count = 1.0 + jax.ops.segment_sum(ones_cut, cut_g, nedge)
    total = jax.ops.segment_sum(zf[cut_row], cut_g, nedge)
    for m in range(MEM):
        count = count + jax.ops.segment_sum(ones_seg, inner_g[:, m], nedge)
        total = total + jax.ops.segment_sum(zf, inner_g[:, m], nedge)
    scale = (edge_weight / count)[:, None]
    edge_val = lax.optimization_barrier((scale * total).astype(jnp.bfloat16)).astype(jnp.float32)
    degree = (MEM + jax.ops.segment_sum(ones_cut, cut_row, nseg))[:, None]
    ysum = jax.ops.segment_sum(edge_val[cut_g], cut_row, nseg)
    for m in range(MEM):
        ysum = ysum + edge_val[inner_g[:, m]]
    y = ysum / degree
    sig_y = jax.nn.sigmoid(y)
    block_out = (y * sig_y).astype(jnp.bfloat16)
    dy = cotangent.astype(jnp.float32) * sig_y * (1.0 + y * (1.0 - sig_y))
    grad_rows = lax.optimization_barrier((dy / degree).astype(jnp.bfloat16)).astype(jnp.float32)
    dtotal = jax.ops.segment_sum(grad_rows[cut_row], cut_g, nedge)
    for m in range(MEM):
        dtotal = dtotal + jax.ops.segment_sum(grad_rows, inner_g[:, m], nedge)
    dedge = lax.optimization_barrier((scale * dtotal).astype(jnp.bfloat16)).astype(jnp.float32)
    dzsum = jax.ops.segment_sum(dedge[cut_g], cut_row, nseg)
    for m in range(MEM):
        dzsum = dzsum + dedge[inner_g[:, m]]
    dz = dzsum.astype(jnp.bfloat16).reshape(nblk, SEG_DEV, -1)
    dx, g_conv, g_bias, g_theta = lax.map(lambda pair: backward_block(pair[0], pair[1], conv_weight, conv_bias, theta), (xs, dz))
    norm = 1.0 / jnp.sqrt(jnp.float32(nseg * TP * B))
    return (block_out, dx.reshape(nseg, -1), lax.optimization_barrier(jnp.sum(g_conv, axis=0)) * norm, lax.optimization_barrier(jnp.sum(g_bias, axis=0)) * norm, lax.optimization_barrier(jnp.sum(g_theta, axis=0)) * norm)
```

```python
import jax
import jax.numpy as jnp
from jax import lax
from jax.sharding import PartitionSpec as P

C = 64
T_SIZE = 12
B = 2
KT = 3
MEM = 2
TP = 10
EDGE_DEV = 128


def device_sum(parts, n):
    sizes = [p.size for p in parts]
    flat = jnp.concatenate([p.reshape(-1) for p in parts])
    if n & (n - 1):
        flat = lax.psum(flat, ("region", "sub"))
    else:
        step = 1
        while step < n:
            perm = [(i, i ^ step) for i in range(n)]
            flat = flat + lax.ppermute(flat, ("region", "sub"), perm)
            step *= 2
    out, at = [], 0
    for p, size in zip(parts, sizes):
        out.append(flat[at : at + size].reshape(p.shape))
        at += size
    return out


def body(
    feats,
    conv_weight,
    conv_bias,
    theta,
    edge_weight,
    inner_edge,
    crossing_segment,
    cut_dest,
    crossing_hyperedge,
    cotangent,
):
    seg = feats.shape[0]
    n_region = lax.axis_size("region")
    n_sub = lax.axis_size("sub")
    device_list = n_region * n_sub
    slot_capacity = max(2, 2 * crossing_segment.shape[0] // device_list)
    slot_total = device_list * slot_capacity
    width = TP * B * C
    x4 = feats.reshape(seg, T_SIZE, B, C)
    stack = jnp.concatenate([x4[:, k : k + TP] for k in range(KT)], axis=-1)
    u = (
        jnp.einsum("stbk,kf->stbf", stack, conv_weight, preferred_element_type=jnp.float32)
        + conv_bias
    )
    gate = jax.nn.sigmoid(u[..., C:])
    first = u[..., :C]
    hidden = (first * gate).astype(jnp.bfloat16)
    z = (
        jnp.einsum("stbc,cd->stbd", hidden, theta, preferred_element_type=jnp.float32)
        .astype(jnp.bfloat16)
        .reshape(seg, width)
    )
    edge_index = jnp.arange(EDGE_DEV, dtype=jnp.int32)
    incidence = jnp.zeros((EDGE_DEV, seg), jnp.float32)
    for m in range(MEM):
        incidence = incidence + (inner_edge[:, m][None, :] == edge_index[:, None]).astype(
            jnp.float32
        )
    inner_count = jnp.sum(incidence, axis=1)
    incidence = incidence.astype(jnp.bfloat16)
    dest = cut_dest[:, 0]
    dest_hot = (dest[:, None] == jnp.arange(device_list, dtype=jnp.int32)[None, :]).astype(
        jnp.int32
    )
    rank = jnp.sum((jnp.cumsum(dest_hot, axis=0) - 1) * dest_hot, axis=1)
    slot_position = dest * slot_capacity + rank
    slotted_segment = jnp.full((slot_total,), -1, jnp.int32).at[slot_position].set(crossing_segment)
    slotted_hyperedge = (
        jnp.full((slot_total,), -1, jnp.int32).at[slot_position].set(crossing_hyperedge)
    )
    members = (slotted_segment[None, :] == jnp.arange(seg, dtype=jnp.int32)[:, None]).astype(
        jnp.float32
    )
    degree = (MEM + jnp.sum(members, axis=1))[:, None]
    members = members.astype(jnp.bfloat16)

    def pick_slots(rows):
        return jnp.einsum("sn,sf->nf", members, rows, preferred_element_type=jnp.float32).astype(
            jnp.bfloat16
        )

    send = pick_slots(z)
    recv, recv_edge = (
        lax.all_to_all(send, ("region", "sub"), split_axis=0, concat_axis=0, tiled=True),
        lax.all_to_all(
            slotted_hyperedge, ("region", "sub"), split_axis=0, concat_axis=0, tiled=True
        ),
    )
    owned = (recv_edge[None, :] == edge_index[:, None]).astype(jnp.float32)
    count = 1.0 + inner_count + jnp.sum(owned, axis=1)
    owned = owned.astype(jnp.bfloat16)
    scale = (edge_weight / count)[:, None]

    def edge_side(local_rows, arrived):
        total = jnp.dot(incidence, local_rows, preferred_element_type=jnp.float32) + jnp.dot(
            owned, arrived, preferred_element_type=jnp.float32
        )
        values = (scale * total).astype(jnp.bfloat16)
        returned = jnp.einsum(
            "en,ef->nf", owned, values, preferred_element_type=jnp.float32
        ).astype(jnp.bfloat16)
        return (values, returned)

    def member_side(values, back):
        return jnp.einsum(
            "es,ef->sf", incidence, values, preferred_element_type=jnp.float32
        ) + jnp.dot(members, back, preferred_element_type=jnp.float32)

    edge_val, ret_rows = edge_side(z, recv)
    back = lax.all_to_all(ret_rows, ("region", "sub"), split_axis=0, concat_axis=0, tiled=True)
    y = member_side(edge_val, back) / degree
    sig_y = jax.nn.sigmoid(y)
    block_out = (y * sig_y).astype(jnp.bfloat16)
    dy = cotangent.astype(jnp.float32) * sig_y * (1.0 + y * (1.0 - sig_y))
    grad_rows = (dy / degree).astype(jnp.bfloat16)
    send_grads = pick_slots(grad_rows)
    recv_grads = lax.all_to_all(
        send_grads, ("region", "sub"), split_axis=0, concat_axis=0, tiled=True
    )
    dedge, ret_grads = edge_side(grad_rows, recv_grads)
    back_grads = lax.all_to_all(
        ret_grads, ("region", "sub"), split_axis=0, concat_axis=0, tiled=True
    )
    dz = member_side(dedge, back_grads).astype(jnp.bfloat16).reshape(seg, TP, B, C)
    g_theta = jnp.einsum("stbc,stbd->cd", hidden, dz, preferred_element_type=jnp.float32)
    dh = jnp.einsum("stbd,cd->stbc", dz, theta, preferred_element_type=jnp.float32)
    du = jnp.concatenate([dh * gate, dh * first * gate * (1.0 - gate)], axis=-1).astype(
        jnp.bfloat16
    )
    g_conv = jnp.einsum("stbk,stbf->kf", stack, du, preferred_element_type=jnp.float32)
    g_bias = jnp.sum(du.astype(jnp.float32), axis=(0, 1, 2))
    sum_conv, sum_bias, sum_theta = device_sum((g_conv, g_bias, g_theta), device_list)
    norm = 1.0 / jnp.sqrt(jnp.float32(seg * device_list * TP * B))
    dstack = jnp.einsum("stbf,kf->stbk", du, conv_weight, preferred_element_type=jnp.float32)
    grad_sum = jnp.zeros((seg, T_SIZE, B, C), jnp.float32)
    for k in range(KT):
        grad_sum = grad_sum + jnp.pad(
            dstack[..., k * C : (k + 1) * C], ((0, 0), (k, KT - 1 - k), (0, 0), (0, 0))
        )
    grad_feats = grad_sum.astype(jnp.bfloat16).reshape(seg, T_SIZE * B * C)
    return (block_out, grad_feats, sum_conv * norm, sum_bias * norm, sum_theta * norm)


def solution(mesh):
    in_specs = (
        P(("region", "sub"), None),
        P(),
        P(),
        P(),
        P(("region", "sub")),
        P(("region", "sub"), None),
        P(("region", "sub")),
        P(("region", "sub"), None),
        P(("region", "sub")),
        P(("region", "sub"), None),
    )
    out_specs = (P(("region", "sub"), None), P(("region", "sub"), None), P(), P(), P())
    return jax.shard_map(body, mesh=mesh, in_specs=in_specs, out_specs=out_specs, check_vma=False)
```

```python
import jax
import jax.numpy as jnp
from jax import lax
from jax.sharding import PartitionSpec as P

C = 64
T_SIZE = 12
B = 2
KT = 3
MEM = 2
TP = 10
EDGE_DEV = 128


def device_sum(parts, n):
    sizes = [p.size for p in parts]
    flat = jnp.concatenate([p.reshape(-1) for p in parts])
    if n & (n - 1):
        flat = lax.psum(flat, ("region", "sub"))
    else:
        step = 1
        while step < n:
            perm = [(i, i ^ step) for i in range(n)]
            flat = flat + lax.ppermute(flat, ("region", "sub"), perm)
            step *= 2
    out, at = [], 0
    for p, size in zip(parts, sizes):
        out.append(flat[at : at + size].reshape(p.shape))
        at += size
    return out


def body(
    feats,
    conv_weight,
    conv_bias,
    theta,
    edge_weight,
    inner_edge,
    crossing_segment,
    cut_dest,
    crossing_hyperedge,
    cotangent,
):
    seg = feats.shape[0]
    n_region = lax.axis_size("region")
    n_sub = lax.axis_size("sub")
    device_list = n_region * n_sub
    slot_capacity = max(2, 2 * crossing_segment.shape[0] // device_list)
    slot_total = device_list * slot_capacity
    width = TP * B * C
    def front(rows):
        n = rows.shape[0]
        x4 = rows.reshape(n, T_SIZE, B, C)
        stack = jnp.concatenate([x4[:, k : k + TP] for k in range(KT)], axis=-1)
        u = (
            jnp.einsum("stbk,kf->stbf", stack, conv_weight, preferred_element_type=jnp.float32)
            + conv_bias
        )
        gate = jax.nn.sigmoid(u[..., C:])
        first = u[..., :C]
        hidden = (first * gate).astype(jnp.bfloat16)
        z = (
            jnp.einsum("stbc,cd->stbd", hidden, theta, preferred_element_type=jnp.float32)
            .astype(jnp.bfloat16)
            .reshape(n, width)
        )
        return stack, gate, first, hidden, z

    edge_index = jnp.arange(EDGE_DEV, dtype=jnp.int32)
    incidence = jnp.zeros((EDGE_DEV, seg), jnp.float32)
    for m in range(MEM):
        incidence = incidence + (inner_edge[:, m][None, :] == edge_index[:, None]).astype(
            jnp.float32
        )
    inner_count = jnp.sum(incidence, axis=1)
    incidence = incidence.astype(jnp.bfloat16)
    dest = cut_dest[:, 0]
    dest_hot = (dest[:, None] == jnp.arange(device_list, dtype=jnp.int32)[None, :]).astype(
        jnp.int32
    )
    rank = jnp.sum((jnp.cumsum(dest_hot, axis=0) - 1) * dest_hot, axis=1)
    slot_position = dest * slot_capacity + rank
    slotted_segment = jnp.full((slot_total,), -1, jnp.int32).at[slot_position].set(crossing_segment)
    slotted_hyperedge = (
        jnp.full((slot_total,), -1, jnp.int32).at[slot_position].set(crossing_hyperedge)
    )
    members = (slotted_segment[None, :] == jnp.arange(seg, dtype=jnp.int32)[:, None]).astype(
        jnp.float32
    )
    degree = (MEM + jnp.sum(members, axis=1))[:, None]
    members = members.astype(jnp.bfloat16)
    cut_rows = jnp.take(feats, jnp.clip(slotted_segment, 0, seg - 1), axis=0)
    z_slots = front(cut_rows)[4]
    stack, gate, first, hidden, z = front(feats)

    def pick_slots(rows):
        return jnp.einsum("sn,sf->nf", members, rows, preferred_element_type=jnp.float32).astype(
            jnp.bfloat16
        )

    edge_cols = jnp.broadcast_to(slotted_hyperedge.astype(jnp.bfloat16)[:, None], (slot_total, 128))
    send = jnp.concatenate([z_slots, edge_cols], axis=1)
    recv_all = lax.all_to_all(send, ("region", "sub"), split_axis=0, concat_axis=0, tiled=True)
    recv = recv_all[:, :width]
    recv_edge = recv_all[:, width].astype(jnp.int32)
    owned = (recv_edge[None, :] == edge_index[:, None]).astype(jnp.float32)
    count = 1.0 + inner_count + jnp.sum(owned, axis=1)
    owned = owned.astype(jnp.bfloat16)
    scale = (edge_weight / count)[:, None]

    def edge_side(local_rows, arrived):
        total = jnp.dot(incidence, local_rows, preferred_element_type=jnp.float32) + jnp.dot(
            owned, arrived, preferred_element_type=jnp.float32
        )
        values = (scale * total).astype(jnp.bfloat16)
        returned = jnp.einsum(
            "en,ef->nf", owned, values, preferred_element_type=jnp.float32
        ).astype(jnp.bfloat16)
        return (values, returned)

    def member_side(values, back):
        return jnp.einsum(
            "es,ef->sf", incidence, values, preferred_element_type=jnp.float32
        ) + jnp.dot(members, back, preferred_element_type=jnp.float32)

    edge_val, ret_rows = edge_side(z, recv)
    back = lax.all_to_all(ret_rows, ("region", "sub"), split_axis=0, concat_axis=0, tiled=True)
    y = member_side(edge_val, back) / degree
    sig_y = jax.nn.sigmoid(y)
    block_out = (y * sig_y).astype(jnp.bfloat16)
    dy = cotangent.astype(jnp.float32) * sig_y * (1.0 + y * (1.0 - sig_y))
    grad_rows = (dy / degree).astype(jnp.bfloat16)
    send_grads = pick_slots(grad_rows)
    recv_grads = lax.all_to_all(
        send_grads, ("region", "sub"), split_axis=0, concat_axis=0, tiled=True
    )
    dedge, ret_grads = edge_side(grad_rows, recv_grads)
    back_grads = lax.all_to_all(
        ret_grads, ("region", "sub"), split_axis=0, concat_axis=0, tiled=True
    )
    dz = member_side(dedge, back_grads).astype(jnp.bfloat16).reshape(seg, TP, B, C)
    g_theta = jnp.einsum("stbc,stbd->cd", hidden, dz, preferred_element_type=jnp.float32)
    dh = jnp.einsum("stbd,cd->stbc", dz, theta, preferred_element_type=jnp.float32)
    du = jnp.concatenate([dh * gate, dh * first * gate * (1.0 - gate)], axis=-1).astype(
        jnp.bfloat16
    )
    g_conv = jnp.einsum("stbk,stbf->kf", stack, du, preferred_element_type=jnp.float32)
    g_bias = jnp.sum(du.astype(jnp.float32), axis=(0, 1, 2))
    sum_conv, sum_bias, sum_theta = device_sum((g_conv, g_bias, g_theta), device_list)
    norm = 1.0 / jnp.sqrt(jnp.float32(seg * device_list * TP * B))
    dstack = jnp.einsum("stbf,kf->stbk", du, conv_weight, preferred_element_type=jnp.float32)
    grad_sum = jnp.zeros((seg, T_SIZE, B, C), jnp.float32)
    for k in range(KT):
        grad_sum = grad_sum + jnp.pad(
            dstack[..., k * C : (k + 1) * C], ((0, 0), (k, KT - 1 - k), (0, 0), (0, 0))
        )
    grad_feats = grad_sum.astype(jnp.bfloat16).reshape(seg, T_SIZE * B * C)
    return (block_out, grad_feats, sum_conv * norm, sum_bias * norm, sum_theta * norm)


def solution(mesh):
    in_specs = (
        P(("region", "sub"), None),
        P(),
        P(),
        P(),
        P(("region", "sub")),
        P(("region", "sub"), None),
        P(("region", "sub")),
        P(("region", "sub"), None),
        P(("region", "sub")),
        P(("region", "sub"), None),
    )
    out_specs = (P(("region", "sub"), None), P(("region", "sub"), None), P(), P(), P())
    return jax.shard_map(body, mesh=mesh, in_specs=in_specs, out_specs=out_specs, check_vma=False)
```

```python
import jax
import jax.numpy as jnp
from jax import lax
from jax.sharding import PartitionSpec as P

C = 64
T_SIZE = 12
B = 2
KT = 3
MEM = 2
TP = 10
EDGE_DEV = 128


def device_sum(parts, n):
    sizes = [p.size for p in parts]
    flat = jnp.concatenate([p.reshape(-1) for p in parts])
    if n & (n - 1):
        flat = lax.psum(flat, ("region", "sub"))
    else:
        step = 1
        while step < n:
            perm = [(i, i ^ step) for i in range(n)]
            flat = flat + lax.ppermute(flat, ("region", "sub"), perm)
            step *= 2
    out, at = [], 0
    for p, size in zip(parts, sizes):
        out.append(flat[at : at + size].reshape(p.shape))
        at += size
    return out


def body(
    feats,
    conv_weight,
    conv_bias,
    theta,
    edge_weight,
    inner_edge,
    crossing_segment,
    cut_dest,
    crossing_hyperedge,
    cotangent,
):
    seg = feats.shape[0]
    n_region = lax.axis_size("region")
    n_sub = lax.axis_size("sub")
    device_list = n_region * n_sub
    slot_capacity = max(2, 2 * crossing_segment.shape[0] // device_list)
    slot_total = device_list * slot_capacity
    width = TP * B * C
    def front(rows):
        n = rows.shape[0]
        x4 = rows.reshape(n, T_SIZE, B, C)
        stack = jnp.concatenate([x4[:, k : k + TP] for k in range(KT)], axis=-1)
        u = (
            jnp.einsum("stbk,kf->stbf", stack, conv_weight, preferred_element_type=jnp.float32)
            + conv_bias
        )
        gate = jax.nn.sigmoid(u[..., C:])
        first = u[..., :C]
        hidden = (first * gate).astype(jnp.bfloat16)
        z = (
            jnp.einsum("stbc,cd->stbd", hidden, theta, preferred_element_type=jnp.float32)
            .astype(jnp.bfloat16)
            .reshape(n, width)
        )
        return stack, gate, first, hidden, z

    edge_index = jnp.arange(EDGE_DEV, dtype=jnp.int32)
    incidence = jnp.zeros((EDGE_DEV, seg), jnp.float32)
    for m in range(MEM):
        incidence = incidence + (inner_edge[:, m][None, :] == edge_index[:, None]).astype(
            jnp.float32
        )
    inner_count = jnp.sum(incidence, axis=1)
    incidence = incidence.astype(jnp.bfloat16)
    dest = cut_dest[:, 0]
    dest_hot = (dest[:, None] == jnp.arange(device_list, dtype=jnp.int32)[None, :]).astype(
        jnp.int32
    )
    rank = jnp.sum((jnp.cumsum(dest_hot, axis=0) - 1) * dest_hot, axis=1)
    slot_position = dest * slot_capacity + rank
    slotted_segment = jnp.full((slot_total,), -1, jnp.int32).at[slot_position].set(crossing_segment)
    slotted_hyperedge = (
        jnp.full((slot_total,), -1, jnp.int32).at[slot_position].set(crossing_hyperedge)
    )
    members = (slotted_segment[None, :] == jnp.arange(seg, dtype=jnp.int32)[:, None]).astype(
        jnp.float32
    )
    degree = (MEM + jnp.sum(members, axis=1))[:, None]
    members = members.astype(jnp.bfloat16)
    cut_rows = jnp.take(feats, jnp.clip(slotted_segment, 0, seg - 1), axis=0)
    stack, gate, first, hidden, z = front(feats)

    def pick_slots(rows):
        return jnp.einsum("sn,sf->nf", members, rows, preferred_element_type=jnp.float32).astype(
            jnp.bfloat16
        )

    edge_cols = jnp.broadcast_to(slotted_hyperedge.astype(jnp.bfloat16)[:, None], (slot_total, 128))
    in_width = feats.shape[1]
    send = jnp.concatenate([cut_rows, edge_cols], axis=1)
    recv_all = lax.all_to_all(send, ("region", "sub"), split_axis=0, concat_axis=0, tiled=True)
    r_stack, r_gate, r_first, r_hidden, recv = front(recv_all[:, :in_width])
    recv_edge = recv_all[:, in_width].astype(jnp.int32)
    owned = (recv_edge[None, :] == edge_index[:, None]).astype(jnp.float32)
    count = 1.0 + inner_count + jnp.sum(owned, axis=1)
    owned = owned.astype(jnp.bfloat16)
    scale = (edge_weight / count)[:, None]

    def edge_side(local_rows, arrived):
        total = jnp.dot(incidence, local_rows, preferred_element_type=jnp.float32) + jnp.dot(
            owned, arrived, preferred_element_type=jnp.float32
        )
        values = (scale * total).astype(jnp.bfloat16)
        returned = jnp.einsum(
            "en,ef->nf", owned, values, preferred_element_type=jnp.float32
        ).astype(jnp.bfloat16)
        return (values, returned)

    def member_side(values, back):
        return jnp.einsum(
            "es,ef->sf", incidence, values, preferred_element_type=jnp.float32
        ) + jnp.dot(members, back, preferred_element_type=jnp.float32)

    edge_val, ret_rows = edge_side(z, recv)
    back = lax.all_to_all(ret_rows, ("region", "sub"), split_axis=0, concat_axis=0, tiled=True)
    y = member_side(edge_val, back) / degree
    sig_y = jax.nn.sigmoid(y)
    block_out = (y * sig_y).astype(jnp.bfloat16)
    dy = cotangent.astype(jnp.float32) * sig_y * (1.0 + y * (1.0 - sig_y))
    grad_rows = (dy / degree).astype(jnp.bfloat16)
    send_grads = pick_slots(grad_rows)
    recv_grads = lax.all_to_all(
        send_grads, ("region", "sub"), split_axis=0, concat_axis=0, tiled=True
    )
    dedge, ret_grads = edge_side(grad_rows, recv_grads)
    back_grads = lax.all_to_all(
        ret_grads, ("region", "sub"), split_axis=0, concat_axis=0, tiled=True
    )
    dz = member_side(dedge, back_grads).astype(jnp.bfloat16).reshape(seg, TP, B, C)

    def weight_grads(st, gt, fi, hi, dzr):
        g_theta = jnp.einsum("stbc,stbd->cd", hi, dzr, preferred_element_type=jnp.float32)
        dh = jnp.einsum("stbd,cd->stbc", dzr, theta, preferred_element_type=jnp.float32)
        du = jnp.concatenate([dh * gt, dh * fi * gt * (1.0 - gt)], axis=-1).astype(jnp.bfloat16)
        g_conv = jnp.einsum("stbk,stbf->kf", st, du, preferred_element_type=jnp.float32)
        g_bias = jnp.sum(du.astype(jnp.float32), axis=(0, 1, 2))
        return du, g_conv, g_bias, g_theta

    dz_inner = (
        jnp.einsum("es,ef->sf", incidence, dedge, preferred_element_type=jnp.float32)
        .astype(jnp.bfloat16)
        .reshape(seg, TP, B, C)
    )
    _, ga_conv, ga_bias, ga_theta = weight_grads(stack, gate, first, hidden, dz_inner)
    dz_slots = ret_grads.reshape(slot_total, TP, B, C)
    _, gb_conv, gb_bias, gb_theta = weight_grads(r_stack, r_gate, r_first, r_hidden, dz_slots)
    sum_conv, sum_bias, sum_theta = device_sum(
        (ga_conv + gb_conv, ga_bias + gb_bias, ga_theta + gb_theta), device_list
    )
    dh = jnp.einsum("stbd,cd->stbc", dz, theta, preferred_element_type=jnp.float32)
    du = jnp.concatenate([dh * gate, dh * first * gate * (1.0 - gate)], axis=-1).astype(
        jnp.bfloat16
    )
    norm = 1.0 / jnp.sqrt(jnp.float32(seg * device_list * TP * B))
    dstack = jnp.einsum("stbf,kf->stbk", du, conv_weight, preferred_element_type=jnp.float32)
    grad_sum = jnp.zeros((seg, T_SIZE, B, C), jnp.float32)
    for k in range(KT):
        grad_sum = grad_sum + jnp.pad(
            dstack[..., k * C : (k + 1) * C], ((0, 0), (k, KT - 1 - k), (0, 0), (0, 0))
        )
    grad_feats = grad_sum.astype(jnp.bfloat16).reshape(seg, T_SIZE * B * C)
    return (block_out, grad_feats, sum_conv * norm, sum_bias * norm, sum_theta * norm)


def solution(mesh):
    in_specs = (
        P(("region", "sub"), None),
        P(),
        P(),
        P(),
        P(("region", "sub")),
        P(("region", "sub"), None),
        P(("region", "sub")),
        P(("region", "sub"), None),
        P(("region", "sub")),
        P(("region", "sub"), None),
    )
    out_specs = (P(("region", "sub"), None), P(("region", "sub"), None), P(), P(), P())
    return jax.shard_map(body, mesh=mesh, in_specs=in_specs, out_specs=out_specs, check_vma=False)
```

```python
import jax
import jax.numpy as jnp
from jax import lax
from jax.sharding import PartitionSpec as P

C = 64
T_SIZE = 12
B = 2
KT = 3
MEM = 2
TP = 10
EDGE_DEV = 128


def device_sum(parts, n):
    sizes = [p.size for p in parts]
    flat = jnp.concatenate([p.reshape(-1) for p in parts])
    if n & (n - 1):
        flat = lax.psum(flat, ("region", "sub"))
    else:
        step = 1
        while step < n:
            perm = [(i, i ^ step) for i in range(n)]
            flat = flat + lax.ppermute(flat, ("region", "sub"), perm)
            step *= 2
    out, at = [], 0
    for p, size in zip(parts, sizes):
        out.append(flat[at : at + size].reshape(p.shape))
        at += size
    return out


def body(
    feats,
    conv_weight,
    conv_bias,
    theta,
    edge_weight,
    inner_edge,
    crossing_segment,
    cut_dest,
    crossing_hyperedge,
    cotangent,
):
    seg = feats.shape[0]
    n_region = lax.axis_size("region")
    n_sub = lax.axis_size("sub")
    device_list = n_region * n_sub
    slot_capacity = max(2, 2 * crossing_segment.shape[0] // device_list)
    slot_total = device_list * slot_capacity
    width = TP * B * C
    def front(rows):
        n = rows.shape[0]
        x4 = rows.reshape(n, T_SIZE, B, C)
        stack = jnp.concatenate([x4[:, k : k + TP] for k in range(KT)], axis=-1)
        u = (
            jnp.einsum("stbk,kf->stbf", stack, conv_weight, preferred_element_type=jnp.float32)
            + conv_bias
        )
        gate = jax.nn.sigmoid(u[..., C:])
        first = u[..., :C]
        hidden = (first * gate).astype(jnp.bfloat16)
        z = (
            jnp.einsum("stbc,cd->stbd", hidden, theta, preferred_element_type=jnp.float32)
            .astype(jnp.bfloat16)
            .reshape(n, width)
        )
        return stack, gate, first, hidden, z

    edge_index = jnp.arange(EDGE_DEV, dtype=jnp.int32)
    incidence = jnp.zeros((EDGE_DEV, seg), jnp.float32)
    for m in range(MEM):
        incidence = incidence + (inner_edge[:, m][None, :] == edge_index[:, None]).astype(
            jnp.float32
        )
    inner_count = jnp.sum(incidence, axis=1)
    incidence = incidence.astype(jnp.bfloat16)
    dest = cut_dest[:, 0]
    dest_hot = (dest[:, None] == jnp.arange(device_list, dtype=jnp.int32)[None, :]).astype(
        jnp.int32
    )
    rank = jnp.sum((jnp.cumsum(dest_hot, axis=0) - 1) * dest_hot, axis=1)
    slot_position = dest * slot_capacity + rank
    slotted_segment = jnp.full((slot_total,), -1, jnp.int32).at[slot_position].set(crossing_segment)
    slotted_hyperedge = (
        jnp.full((slot_total,), -1, jnp.int32).at[slot_position].set(crossing_hyperedge)
    )
    members = (slotted_segment[None, :] == jnp.arange(seg, dtype=jnp.int32)[:, None]).astype(
        jnp.float32
    )
    degree = (MEM + jnp.sum(members, axis=1))[:, None]
    members = members.astype(jnp.bfloat16)
    cut_rows = jnp.take(feats, jnp.clip(slotted_segment, 0, seg - 1), axis=0)
    stack, gate, first, hidden, z = front(feats)

    def pick_slots(rows):
        return jnp.einsum("sn,sf->nf", members, rows, preferred_element_type=jnp.float32).astype(
            jnp.bfloat16
        )

    edge_cols = jnp.broadcast_to(slotted_hyperedge.astype(jnp.bfloat16)[:, None], (slot_total, 128))
    in_width = feats.shape[1]
    send = jnp.concatenate([cut_rows, edge_cols], axis=1)
    recv_all = lax.all_to_all(send, ("region", "sub"), split_axis=0, concat_axis=0, tiled=True)
    r_stack, r_gate, r_first, r_hidden, recv = front(recv_all[:, :in_width])
    recv_edge = recv_all[:, in_width].astype(jnp.int32)
    owned = (recv_edge[None, :] == edge_index[:, None]).astype(jnp.float32)
    count = 1.0 + inner_count + jnp.sum(owned, axis=1)
    owned = owned.astype(jnp.bfloat16)
    scale = (edge_weight / count)[:, None]

    def edge_side(local_rows, arrived):
        total = jnp.dot(incidence, local_rows, preferred_element_type=jnp.float32) + jnp.dot(
            owned, arrived, preferred_element_type=jnp.float32
        )
        values = (scale * total).astype(jnp.bfloat16)
        returned = jnp.einsum(
            "en,ef->nf", owned, values, preferred_element_type=jnp.float32
        ).astype(jnp.bfloat16)
        return (values, returned)

    def member_side(values, back):
        return jnp.einsum(
            "es,ef->sf", incidence, values, preferred_element_type=jnp.float32
        ) + jnp.dot(members, back, preferred_element_type=jnp.float32)

    edge_val, ret_rows = edge_side(z, recv)
    back = lax.all_to_all(ret_rows, ("region", "sub"), split_axis=0, concat_axis=0, tiled=True)
    y = member_side(edge_val, back) / degree
    sig_y = jax.nn.sigmoid(y)
    block_out = (y * sig_y).astype(jnp.bfloat16)
    dy = cotangent.astype(jnp.float32) * sig_y * (1.0 + y * (1.0 - sig_y))
    grad_rows = (dy / degree).astype(jnp.bfloat16)
    send_grads = pick_slots(grad_rows)
    recv_grads = lax.all_to_all(
        send_grads, ("region", "sub"), split_axis=0, concat_axis=0, tiled=True
    )
    dedge, ret_grads = edge_side(grad_rows, recv_grads)
    inner_sum = jnp.einsum("es,ef->sf", incidence, dedge, preferred_element_type=jnp.float32)
    inner_sum, ret_grads = lax.optimization_barrier((inner_sum, ret_grads))
    back_grads = lax.all_to_all(
        ret_grads, ("region", "sub"), split_axis=0, concat_axis=0, tiled=True
    )

    def weight_grads(st, gt, fi, hi, dzr):
        g_theta = jnp.einsum("stbc,stbd->cd", hi, dzr, preferred_element_type=jnp.float32)
        dh = jnp.einsum("stbd,cd->stbc", dzr, theta, preferred_element_type=jnp.float32)
        du = jnp.concatenate([dh * gt, dh * fi * gt * (1.0 - gt)], axis=-1).astype(jnp.bfloat16)
        g_conv = jnp.einsum("stbk,stbf->kf", st, du, preferred_element_type=jnp.float32)
        g_bias = jnp.sum(du.astype(jnp.float32), axis=(0, 1, 2))
        return du, g_conv, g_bias, g_theta

    dz_inner = inner_sum.astype(jnp.bfloat16).reshape(seg, TP, B, C)
    _, ga_conv, ga_bias, ga_theta = weight_grads(stack, gate, first, hidden, dz_inner)
    dz_slots = ret_grads.reshape(slot_total, TP, B, C)
    _, gb_conv, gb_bias, gb_theta = weight_grads(r_stack, r_gate, r_first, r_hidden, dz_slots)
    partial = (ga_conv + gb_conv, ga_bias + gb_bias, ga_theta + gb_theta)
    sum_conv, sum_bias, sum_theta = device_sum(partial, device_list)
    _, back_grads = lax.optimization_barrier((partial, back_grads))
    dz = (
        (inner_sum + jnp.dot(members, back_grads, preferred_element_type=jnp.float32))
        .astype(jnp.bfloat16)
        .reshape(seg, TP, B, C)
    )
    dh = jnp.einsum("stbd,cd->stbc", dz, theta, preferred_element_type=jnp.float32)
    du = jnp.concatenate([dh * gate, dh * first * gate * (1.0 - gate)], axis=-1).astype(
        jnp.bfloat16
    )
    norm = 1.0 / jnp.sqrt(jnp.float32(seg * device_list * TP * B))
    dstack = jnp.einsum("stbf,kf->stbk", du, conv_weight, preferred_element_type=jnp.float32)
    grad_sum = jnp.zeros((seg, T_SIZE, B, C), jnp.float32)
    for k in range(KT):
        grad_sum = grad_sum + jnp.pad(
            dstack[..., k * C : (k + 1) * C], ((0, 0), (k, KT - 1 - k), (0, 0), (0, 0))
        )
    grad_feats = grad_sum.astype(jnp.bfloat16).reshape(seg, T_SIZE * B * C)
    return (block_out, grad_feats, sum_conv * norm, sum_bias * norm, sum_theta * norm)


def solution(mesh):
    in_specs = (
        P(("region", "sub"), None),
        P(),
        P(),
        P(),
        P(("region", "sub")),
        P(("region", "sub"), None),
        P(("region", "sub")),
        P(("region", "sub"), None),
        P(("region", "sub")),
        P(("region", "sub"), None),
    )
    out_specs = (P(("region", "sub"), None), P(("region", "sub"), None), P(), P(), P())
    return jax.shard_map(body, mesh=mesh, in_specs=in_specs, out_specs=out_specs, check_vma=False)
```

```python
import jax
import jax.numpy as jnp
from jax import lax
from jax.sharding import PartitionSpec as P

C = 64
T_SIZE = 12
B = 2
KT = 3
MEM = 2
TP = 10
EDGE_DEV = 128


def device_sum(parts, n):
    sizes = [p.size for p in parts]
    flat = jnp.concatenate([p.reshape(-1) for p in parts])
    if n & (n - 1):
        flat = lax.psum(flat, ("region", "sub"))
    else:
        step = 1
        while step < n:
            perm = [(i, i ^ step) for i in range(n)]
            flat = flat + lax.ppermute(flat, ("region", "sub"), perm)
            step *= 2
    out, at = [], 0
    for p, size in zip(parts, sizes):
        out.append(flat[at : at + size].reshape(p.shape))
        at += size
    return out


def body(
    feats,
    conv_weight,
    conv_bias,
    theta,
    edge_weight,
    inner_edge,
    crossing_segment,
    cut_dest,
    crossing_hyperedge,
    cotangent,
):
    seg = feats.shape[0]
    n_region = lax.axis_size("region")
    n_sub = lax.axis_size("sub")
    device_list = n_region * n_sub
    slot_capacity = max(2, 2 * crossing_segment.shape[0] // device_list)
    slot_total = device_list * slot_capacity
    width = TP * B * C
    def front(rows):
        n = rows.shape[0]
        x4 = rows.reshape(n, T_SIZE, B, C)
        stack = jnp.concatenate([x4[:, k : k + TP] for k in range(KT)], axis=-1)
        u = (
            jnp.einsum("stbk,kf->stbf", stack, conv_weight, preferred_element_type=jnp.float32)
            + conv_bias
        )
        gate = jax.nn.sigmoid(u[..., C:])
        first = u[..., :C]
        hidden = (first * gate).astype(jnp.bfloat16)
        z = (
            jnp.einsum("stbc,cd->stbd", hidden, theta, preferred_element_type=jnp.float32)
            .astype(jnp.bfloat16)
            .reshape(n, width)
        )
        return stack, gate, first, hidden, z

    edge_index = jnp.arange(EDGE_DEV, dtype=jnp.int32)
    incidence = jnp.zeros((EDGE_DEV, seg), jnp.float32)
    for m in range(MEM):
        incidence = incidence + (inner_edge[:, m][None, :] == edge_index[:, None]).astype(
            jnp.float32
        )
    inner_count = jnp.sum(incidence, axis=1)
    incidence = incidence.astype(jnp.bfloat16)
    dest = cut_dest[:, 0]
    dest_hot = (dest[:, None] == jnp.arange(device_list, dtype=jnp.int32)[None, :]).astype(
        jnp.int32
    )
    rank = jnp.sum((jnp.cumsum(dest_hot, axis=0) - 1) * dest_hot, axis=1)
    slot_position = dest * slot_capacity + rank
    slotted_segment = jnp.full((slot_total,), -1, jnp.int32).at[slot_position].set(crossing_segment)
    slotted_hyperedge = (
        jnp.full((slot_total,), -1, jnp.int32).at[slot_position].set(crossing_hyperedge)
    )
    members = (slotted_segment[None, :] == jnp.arange(seg, dtype=jnp.int32)[:, None]).astype(
        jnp.float32
    )
    degree = (MEM + jnp.sum(members, axis=1))[:, None]
    members = members.astype(jnp.bfloat16)
    cut_rows = jnp.take(feats, jnp.clip(slotted_segment, 0, seg - 1), axis=0)
    stack, gate, first, hidden, z = front(feats)

    def pick_slots(rows):
        return jnp.einsum("sn,sf->nf", members, rows, preferred_element_type=jnp.float32).astype(
            jnp.bfloat16
        )

    edge_cols = jnp.broadcast_to(slotted_hyperedge.astype(jnp.bfloat16)[:, None], (slot_total, 128))
    in_width = feats.shape[1]
    send = jnp.concatenate([cut_rows, edge_cols], axis=1)
    recv_all = lax.all_to_all(send, ("region", "sub"), split_axis=0, concat_axis=0, tiled=True)
    r_stack, r_gate, r_first, r_hidden, recv = front(recv_all[:, :in_width])
    recv_edge = recv_all[:, in_width].astype(jnp.int32)
    owned = (recv_edge[None, :] == edge_index[:, None]).astype(jnp.float32)
    count = 1.0 + inner_count + jnp.sum(owned, axis=1)
    owned = owned.astype(jnp.bfloat16)
    scale = (edge_weight / count)[:, None]

    def edge_side(local_rows, arrived):
        total = jnp.dot(incidence, local_rows, preferred_element_type=jnp.float32) + jnp.dot(
            owned, arrived, preferred_element_type=jnp.float32
        )
        values = (scale * total).astype(jnp.bfloat16)
        returned = jnp.einsum(
            "en,ef->nf", owned, values, preferred_element_type=jnp.float32
        ).astype(jnp.bfloat16)
        return (values, returned)

    def member_side(values, back):
        return jnp.einsum(
            "es,ef->sf", incidence, values, preferred_element_type=jnp.float32
        ) + jnp.dot(members, back, preferred_element_type=jnp.float32)

    edge_val, ret_rows = edge_side(z, recv)
    back = lax.all_to_all(ret_rows, ("region", "sub"), split_axis=0, concat_axis=0, tiled=True)
    y = member_side(edge_val, back) / degree
    sig_y = jax.nn.sigmoid(y)
    block_out = (y * sig_y).astype(jnp.bfloat16)
    dy = cotangent.astype(jnp.float32) * sig_y * (1.0 + y * (1.0 - sig_y))
    grad_rows = (dy / degree).astype(jnp.bfloat16)
    send_grads = pick_slots(grad_rows)
    recv_grads = lax.all_to_all(
        send_grads, ("region", "sub"), split_axis=0, concat_axis=0, tiled=True
    )
    dedge, ret_grads = edge_side(grad_rows, recv_grads)
    inner_sum = jnp.einsum("es,ef->sf", incidence, dedge, preferred_element_type=jnp.float32)
    inner_sum, ret_grads = lax.optimization_barrier((inner_sum, ret_grads))
    back_grads = lax.all_to_all(
        ret_grads, ("region", "sub"), split_axis=0, concat_axis=0, tiled=True
    )

    def weight_grads(st, gt, fi, hi, dzr):
        g_theta = jnp.einsum("stbc,stbd->cd", hi, dzr, preferred_element_type=jnp.float32)
        dh = jnp.einsum("stbd,cd->stbc", dzr, theta, preferred_element_type=jnp.float32)
        du = jnp.concatenate([dh * gt, dh * fi * gt * (1.0 - gt)], axis=-1).astype(jnp.bfloat16)
        g_conv = jnp.einsum("stbk,stbf->kf", st, du, preferred_element_type=jnp.float32)
        g_bias = jnp.sum(du.astype(jnp.float32), axis=(0, 1, 2))
        return du, g_conv, g_bias, g_theta

    dz_inner = inner_sum.astype(jnp.bfloat16).reshape(seg, TP, B, C)
    _, ga_conv, ga_bias, ga_theta = weight_grads(stack, gate, first, hidden, dz_inner)
    dz_slots = ret_grads.reshape(slot_total, TP, B, C)
    _, gb_conv, gb_bias, gb_theta = weight_grads(r_stack, r_gate, r_first, r_hidden, dz_slots)
    partial = (ga_conv + gb_conv, ga_bias + gb_bias, ga_theta + gb_theta)
    partial, back_grads = lax.optimization_barrier((partial, back_grads))
    sum_conv, sum_bias, sum_theta = device_sum(partial, device_list)
    dz = (
        (inner_sum + jnp.dot(members, back_grads, preferred_element_type=jnp.float32))
        .astype(jnp.bfloat16)
        .reshape(seg, TP, B, C)
    )
    dh = jnp.einsum("stbd,cd->stbc", dz, theta, preferred_element_type=jnp.float32)
    du = jnp.concatenate([dh * gate, dh * first * gate * (1.0 - gate)], axis=-1).astype(
        jnp.bfloat16
    )
    norm = 1.0 / jnp.sqrt(jnp.float32(seg * device_list * TP * B))
    dstack = jnp.einsum("stbf,kf->stbk", du, conv_weight, preferred_element_type=jnp.float32)
    grad_sum = jnp.zeros((seg, T_SIZE, B, C), jnp.float32)
    for k in range(KT):
        grad_sum = grad_sum + jnp.pad(
            dstack[..., k * C : (k + 1) * C], ((0, 0), (k, KT - 1 - k), (0, 0), (0, 0))
        )
    grad_feats = grad_sum.astype(jnp.bfloat16).reshape(seg, T_SIZE * B * C)
    return (block_out, grad_feats, sum_conv * norm, sum_bias * norm, sum_theta * norm)


def solution(mesh):
    in_specs = (
        P(("region", "sub"), None),
        P(),
        P(),
        P(),
        P(("region", "sub")),
        P(("region", "sub"), None),
        P(("region", "sub")),
        P(("region", "sub"), None),
        P(("region", "sub")),
        P(("region", "sub"), None),
    )
    out_specs = (P(("region", "sub"), None), P(("region", "sub"), None), P(), P(), P())
    return jax.shard_map(body, mesh=mesh, in_specs=in_specs, out_specs=out_specs, check_vma=False)
```

```python
import jax
import jax.numpy as jnp
from jax import lax
from jax.sharding import PartitionSpec as P

C = 64
T_SIZE = 12
B = 2
KT = 3
MEM = 2
TP = 10
EDGE_DEV = 128


def device_sum(parts, n):
    sizes = [p.size for p in parts]
    flat = jnp.concatenate([p.reshape(-1) for p in parts])
    if n & (n - 1):
        flat = lax.psum(flat, ("region", "sub"))
    else:
        step = 1
        while step < n:
            perm = [(i, i ^ step) for i in range(n)]
            flat = flat + lax.ppermute(flat, ("region", "sub"), perm)
            step *= 2
    out, at = [], 0
    for p, size in zip(parts, sizes):
        out.append(flat[at : at + size].reshape(p.shape))
        at += size
    return out


def body(
    feats,
    conv_weight,
    conv_bias,
    theta,
    edge_weight,
    inner_edge,
    crossing_segment,
    cut_dest,
    crossing_hyperedge,
    cotangent,
):
    seg = feats.shape[0]
    n_region = lax.axis_size("region")
    n_sub = lax.axis_size("sub")
    device_list = n_region * n_sub
    slot_capacity = max(2, 2 * crossing_segment.shape[0] // device_list)
    slot_total = device_list * slot_capacity
    width = TP * B * C
    def front(rows):
        n = rows.shape[0]
        x4 = rows.reshape(n, T_SIZE, B, C)
        stack = jnp.concatenate([x4[:, k : k + TP] for k in range(KT)], axis=-1)
        u = (
            jnp.einsum("stbk,kf->stbf", stack, conv_weight, preferred_element_type=jnp.float32)
            + conv_bias
        )
        gate = jax.nn.sigmoid(u[..., C:])
        first = u[..., :C]
        hidden = (first * gate).astype(jnp.bfloat16)
        z = (
            jnp.einsum("stbc,cd->stbd", hidden, theta, preferred_element_type=jnp.float32)
            .astype(jnp.bfloat16)
            .reshape(n, width)
        )
        return stack, gate, first, hidden, z

    edge_index = jnp.arange(EDGE_DEV, dtype=jnp.int32)
    incidence = jnp.zeros((EDGE_DEV, seg), jnp.float32)
    for m in range(MEM):
        incidence = incidence + (inner_edge[:, m][None, :] == edge_index[:, None]).astype(
            jnp.float32
        )
    inner_count = jnp.sum(incidence, axis=1)
    incidence = incidence.astype(jnp.bfloat16)
    dest = cut_dest[:, 0]
    dest_hot = (dest[:, None] == jnp.arange(device_list, dtype=jnp.int32)[None, :]).astype(
        jnp.int32
    )
    rank = jnp.sum((jnp.cumsum(dest_hot, axis=0) - 1) * dest_hot, axis=1)
    slot_position = dest * slot_capacity + rank
    slotted_segment = jnp.full((slot_total,), -1, jnp.int32).at[slot_position].set(crossing_segment)
    slotted_hyperedge = (
        jnp.full((slot_total,), -1, jnp.int32).at[slot_position].set(crossing_hyperedge)
    )
    members = (slotted_segment[None, :] == jnp.arange(seg, dtype=jnp.int32)[:, None]).astype(
        jnp.float32
    )
    degree = (MEM + jnp.sum(members, axis=1))[:, None]
    members = members.astype(jnp.bfloat16)
    def pick_slots(rows):
        return jnp.einsum("sn,sf->nf", members, rows, preferred_element_type=jnp.float32).astype(
            jnp.bfloat16
        )

    cut_rows = pick_slots(feats)
    stack, gate, first, hidden, z = front(feats)

    edge_cols = jnp.broadcast_to(slotted_hyperedge.astype(jnp.bfloat16)[:, None], (slot_total, 128))
    in_width = feats.shape[1]
    send = jnp.concatenate([cut_rows, edge_cols], axis=1)
    recv_all = lax.all_to_all(send, ("region", "sub"), split_axis=0, concat_axis=0, tiled=True)
    r_stack, r_gate, r_first, r_hidden, recv = front(recv_all[:, :in_width])
    recv_edge = recv_all[:, in_width].astype(jnp.int32)
    owned = (recv_edge[None, :] == edge_index[:, None]).astype(jnp.float32)
    count = 1.0 + inner_count + jnp.sum(owned, axis=1)
    owned = owned.astype(jnp.bfloat16)
    scale = (edge_weight / count)[:, None]

    def edge_side(local_rows, arrived):
        total = jnp.dot(incidence, local_rows, preferred_element_type=jnp.float32) + jnp.dot(
            owned, arrived, preferred_element_type=jnp.float32
        )
        values = (scale * total).astype(jnp.bfloat16)
        returned = jnp.einsum(
            "en,ef->nf", owned, values, preferred_element_type=jnp.float32
        ).astype(jnp.bfloat16)
        return (values, returned)

    def member_side(values, back):
        return jnp.einsum(
            "es,ef->sf", incidence, values, preferred_element_type=jnp.float32
        ) + jnp.dot(members, back, preferred_element_type=jnp.float32)

    edge_val, ret_rows = edge_side(z, recv)
    back = lax.all_to_all(ret_rows, ("region", "sub"), split_axis=0, concat_axis=0, tiled=True)
    y = member_side(edge_val, back) / degree
    sig_y = jax.nn.sigmoid(y)
    block_out = (y * sig_y).astype(jnp.bfloat16)
    dy = cotangent.astype(jnp.float32) * sig_y * (1.0 + y * (1.0 - sig_y))
    grad_rows = (dy / degree).astype(jnp.bfloat16)
    send_grads = pick_slots(grad_rows)
    recv_grads = lax.all_to_all(
        send_grads, ("region", "sub"), split_axis=0, concat_axis=0, tiled=True
    )
    dedge, ret_grads = edge_side(grad_rows, recv_grads)
    inner_sum = jnp.einsum("es,ef->sf", incidence, dedge, preferred_element_type=jnp.float32)
    inner_sum, ret_grads = lax.optimization_barrier((inner_sum, ret_grads))
    back_grads = lax.all_to_all(
        ret_grads, ("region", "sub"), split_axis=0, concat_axis=0, tiled=True
    )

    def weight_grads(st, gt, fi, hi, dzr):
        g_theta = jnp.einsum("stbc,stbd->cd", hi, dzr, preferred_element_type=jnp.float32)
        dh = jnp.einsum("stbd,cd->stbc", dzr, theta, preferred_element_type=jnp.float32)
        du = jnp.concatenate([dh * gt, dh * fi * gt * (1.0 - gt)], axis=-1).astype(jnp.bfloat16)
        g_conv = jnp.einsum("stbk,stbf->kf", st, du, preferred_element_type=jnp.float32)
        g_bias = jnp.sum(du.astype(jnp.float32), axis=(0, 1, 2))
        return du, g_conv, g_bias, g_theta

    dz_inner = inner_sum.astype(jnp.bfloat16).reshape(seg, TP, B, C)
    _, ga_conv, ga_bias, ga_theta = weight_grads(stack, gate, first, hidden, dz_inner)
    dz_slots = ret_grads.reshape(slot_total, TP, B, C)
    _, gb_conv, gb_bias, gb_theta = weight_grads(r_stack, r_gate, r_first, r_hidden, dz_slots)
    partial = (ga_conv + gb_conv, ga_bias + gb_bias, ga_theta + gb_theta)
    partial, back_grads = lax.optimization_barrier((partial, back_grads))
    sum_conv, sum_bias, sum_theta = device_sum(partial, device_list)
    dz = (
        (inner_sum + jnp.dot(members, back_grads, preferred_element_type=jnp.float32))
        .astype(jnp.bfloat16)
        .reshape(seg, TP, B, C)
    )
    dh = jnp.einsum("stbd,cd->stbc", dz, theta, preferred_element_type=jnp.float32)
    du = jnp.concatenate([dh * gate, dh * first * gate * (1.0 - gate)], axis=-1).astype(
        jnp.bfloat16
    )
    norm = 1.0 / jnp.sqrt(jnp.float32(seg * device_list * TP * B))
    dstack = jnp.einsum("stbf,kf->stbk", du, conv_weight, preferred_element_type=jnp.float32)
    grad_sum = jnp.zeros((seg, T_SIZE, B, C), jnp.float32)
    for k in range(KT):
        grad_sum = grad_sum + jnp.pad(
            dstack[..., k * C : (k + 1) * C], ((0, 0), (k, KT - 1 - k), (0, 0), (0, 0))
        )
    grad_feats = grad_sum.astype(jnp.bfloat16).reshape(seg, T_SIZE * B * C)
    return (block_out, grad_feats, sum_conv * norm, sum_bias * norm, sum_theta * norm)


def solution(mesh):
    in_specs = (
        P(("region", "sub"), None),
        P(),
        P(),
        P(),
        P(("region", "sub")),
        P(("region", "sub"), None),
        P(("region", "sub")),
        P(("region", "sub"), None),
        P(("region", "sub")),
        P(("region", "sub"), None),
    )
    out_specs = (P(("region", "sub"), None), P(("region", "sub"), None), P(), P(), P())
    return jax.shard_map(body, mesh=mesh, in_specs=in_specs, out_specs=out_specs, check_vma=False)
```

```python
import jax
import jax.numpy as jnp
from jax import lax
from jax.sharding import PartitionSpec as P

C = 64
T_SIZE = 12
B = 2
KT = 3
MEM = 2
TP = 10
EDGE_DEV = 128


def device_sum(parts, n):
    sizes = [p.size for p in parts]
    flat = jnp.concatenate([p.reshape(-1) for p in parts])
    n_sub = lax.axis_size("sub")
    n_region = n // n_sub
    if n & (n - 1):
        flat = lax.psum(flat, ("region", "sub"))
    else:
        last = n_sub if n_region <= 4 else n
        step = 1
        while step < last:
            perm = [(i, i ^ step) for i in range(n)]
            flat = flat + lax.ppermute(flat, ("region", "sub"), perm)
            step *= 2
    if not n & (n - 1) and n_region <= 4:
        region = lax.axis_index("region")
        got = [flat] + [
            lax.ppermute(flat, ("region", "sub"), [(i, i ^ (m * n_sub)) for i in range(n)])
            for m in range(1, n_region)
        ]
        got = jnp.stack(got)
        total = None
        for i in range(n_region):
            v = lax.dynamic_index_in_dim(got, i ^ region, keepdims=False)
            total = v if total is None else total + v
        flat = total
    out, at = [], 0
    for p, size in zip(parts, sizes):
        out.append(flat[at : at + size].reshape(p.shape))
        at += size
    return out


def body(
    feats,
    conv_weight,
    conv_bias,
    theta,
    edge_weight,
    inner_edge,
    crossing_segment,
    cut_dest,
    crossing_hyperedge,
    cotangent,
):
    seg = feats.shape[0]
    n_region = lax.axis_size("region")
    n_sub = lax.axis_size("sub")
    device_list = n_region * n_sub
    slot_capacity = max(2, 2 * crossing_segment.shape[0] // device_list)
    slot_total = device_list * slot_capacity
    width = TP * B * C
    def front(rows):
        n = rows.shape[0]
        x4 = rows.reshape(n, -1, B, C)
        stack = jnp.concatenate([x4[:, k : k + TP] for k in range(KT)], axis=-1)
        u = (
            jnp.einsum("stbk,kf->stbf", stack, conv_weight, preferred_element_type=jnp.float32)
            + conv_bias
        )
        gate = jax.nn.sigmoid(u[..., C:])
        first = u[..., :C]
        hidden = (first * gate).astype(jnp.bfloat16)
        z = (
            jnp.einsum("stbc,cd->stbd", hidden, theta, preferred_element_type=jnp.float32)
            .astype(jnp.bfloat16)
            .reshape(n, width)
        )
        return stack, gate, first, hidden, z

    edge_index = jnp.arange(EDGE_DEV, dtype=jnp.int32)
    incidence = jnp.zeros((EDGE_DEV, seg), jnp.float32)
    for m in range(MEM):
        incidence = incidence + (inner_edge[:, m][None, :] == edge_index[:, None]).astype(
            jnp.float32
        )
    inner_count = jnp.sum(incidence, axis=1)
    incidence = incidence.astype(jnp.bfloat16)
    dest = cut_dest[:, 0]
    dest_hot = (dest[:, None] == jnp.arange(device_list, dtype=jnp.int32)[None, :]).astype(
        jnp.int32
    )
    rank = jnp.sum((jnp.cumsum(dest_hot, axis=0) - 1) * dest_hot, axis=1)
    slot_position = dest * slot_capacity + rank
    slotted_segment = jnp.full((slot_total,), -1, jnp.int32).at[slot_position].set(crossing_segment)
    slotted_hyperedge = (
        jnp.full((slot_total,), -1, jnp.int32).at[slot_position].set(crossing_hyperedge)
    )
    members = (slotted_segment[None, :] == jnp.arange(seg, dtype=jnp.int32)[:, None]).astype(
        jnp.float32
    )
    degree = (MEM + jnp.sum(members, axis=1))[:, None]
    members = members.astype(jnp.bfloat16)
    def pick_slots(rows):
        return jnp.einsum("sn,sf->nf", members, rows, preferred_element_type=jnp.float32).astype(
            jnp.bfloat16
        )

    cut_rows = pick_slots(feats)
    stack, gate, first, hidden, z = front(feats)

    edge_cols = jnp.broadcast_to(slotted_hyperedge.astype(jnp.bfloat16)[:, None], (slot_total, B * C))
    in_width = feats.shape[1]
    send = jnp.concatenate([cut_rows, edge_cols], axis=1)
    recv_all = lax.all_to_all(send, ("region", "sub"), split_axis=0, concat_axis=0, tiled=True)
    r_stack, r_gate, r_first, r_hidden, recv = front(recv_all)
    recv_edge = recv_all[:, in_width].astype(jnp.int32)
    owned = (recv_edge[None, :] == edge_index[:, None]).astype(jnp.float32)
    count = 1.0 + inner_count + jnp.sum(owned, axis=1)
    owned = owned.astype(jnp.bfloat16)
    scale = (edge_weight / count)[:, None]

    def edge_side(local_rows, arrived):
        total = jnp.dot(incidence, local_rows, preferred_element_type=jnp.float32) + jnp.dot(
            owned, arrived, preferred_element_type=jnp.float32
        )
        values = (scale * total).astype(jnp.bfloat16)
        returned = jnp.einsum(
            "en,ef->nf", owned, values, preferred_element_type=jnp.float32
        ).astype(jnp.bfloat16)
        return (values, returned)

    def member_side(values, back):
        return jnp.einsum(
            "es,ef->sf", incidence, values, preferred_element_type=jnp.float32
        ) + jnp.dot(members, back, preferred_element_type=jnp.float32)

    edge_val, ret_rows = edge_side(z, recv)
    back = lax.all_to_all(ret_rows, ("region", "sub"), split_axis=0, concat_axis=0, tiled=True)
    y = member_side(edge_val, back) / degree
    sig_y = jax.nn.sigmoid(y)
    block_out = (y * sig_y).astype(jnp.bfloat16)
    dy = cotangent.astype(jnp.float32) * sig_y * (1.0 + y * (1.0 - sig_y))
    grad_rows = (dy / degree).astype(jnp.bfloat16)
    send_grads = pick_slots(grad_rows)
    recv_grads = lax.all_to_all(
        send_grads, ("region", "sub"), split_axis=0, concat_axis=0, tiled=True
    )
    dedge, ret_grads = edge_side(grad_rows, recv_grads)
    inner_sum = jnp.einsum("es,ef->sf", incidence, dedge, preferred_element_type=jnp.float32)
    inner_sum, ret_grads = lax.optimization_barrier((inner_sum, ret_grads))
    back_grads = lax.all_to_all(
        ret_grads, ("region", "sub"), split_axis=0, concat_axis=0, tiled=True
    )

    def weight_grads(st, gt, fi, hi, dzr):
        g_theta = jnp.einsum("stbc,stbd->cd", hi, dzr, preferred_element_type=jnp.float32)
        dh = jnp.einsum("stbd,cd->stbc", dzr, theta, preferred_element_type=jnp.float32)
        du = jnp.concatenate([dh * gt, dh * fi * gt * (1.0 - gt)], axis=-1).astype(jnp.bfloat16)
        g_conv = jnp.einsum("stbk,stbf->kf", st, du, preferred_element_type=jnp.float32)
        g_bias = jnp.sum(du.astype(jnp.float32), axis=(0, 1, 2))
        return du, g_conv, g_bias, g_theta

    dz_inner = inner_sum.astype(jnp.bfloat16).reshape(seg, TP, B, C)
    _, ga_conv, ga_bias, ga_theta = weight_grads(stack, gate, first, hidden, dz_inner)
    dz_slots = ret_grads.reshape(slot_total, TP, B, C)
    _, gb_conv, gb_bias, gb_theta = weight_grads(r_stack, r_gate, r_first, r_hidden, dz_slots)
    partial = (ga_conv + gb_conv, ga_bias + gb_bias, ga_theta + gb_theta)
    partial, back_grads = lax.optimization_barrier((partial, back_grads))
    sum_conv, sum_bias, sum_theta = device_sum(partial, device_list)
    dz = (
        (inner_sum + jnp.dot(members, back_grads, preferred_element_type=jnp.float32))
        .astype(jnp.bfloat16)
        .reshape(seg, TP, B, C)
    )
    dh = jnp.einsum("stbd,cd->stbc", dz, theta, preferred_element_type=jnp.float32)
    du = jnp.concatenate([dh * gate, dh * first * gate * (1.0 - gate)], axis=-1).astype(
        jnp.bfloat16
    )
    norm = 1.0 / jnp.sqrt(jnp.float32(seg * device_list * TP * B))
    dstack = jnp.einsum("stbf,kf->stbk", du, conv_weight, preferred_element_type=jnp.float32)
    grad_sum = jnp.zeros((seg, T_SIZE, B, C), jnp.float32)
    for k in range(KT):
        grad_sum = grad_sum + jnp.pad(
            dstack[..., k * C : (k + 1) * C], ((0, 0), (k, KT - 1 - k), (0, 0), (0, 0))
        )
    grad_feats = grad_sum.astype(jnp.bfloat16).reshape(seg, T_SIZE * B * C)
    return (block_out, grad_feats, sum_conv * norm, sum_bias * norm, sum_theta * norm)


def solution(mesh):
    in_specs = (
        P(("region", "sub"), None),
        P(),
        P(),
        P(),
        P(("region", "sub")),
        P(("region", "sub"), None),
        P(("region", "sub")),
        P(("region", "sub"), None),
        P(("region", "sub")),
        P(("region", "sub"), None),
    )
    out_specs = (P(("region", "sub"), None), P(("region", "sub"), None), P(), P(), P())
    return jax.shard_map(body, mesh=mesh, in_specs=in_specs, out_specs=out_specs, check_vma=False)
```

```python
import jax
import jax.numpy as jnp
from jax import lax
from jax.sharding import PartitionSpec as P

C = 64
T_SIZE = 12
B = 2
KT = 3
MEM = 2
TP = 10
EDGE_DEV = 128


def device_sum(parts, n):
    sizes = [p.size for p in parts]
    flat = jnp.concatenate([p.reshape(-1) for p in parts])
    if n & (n - 1):
        flat = lax.psum(flat, ("region", "sub"))
    else:
        step = 1
        while step < n:
            perm = [(i, i ^ step) for i in range(n)]
            flat = flat + lax.ppermute(flat, ("region", "sub"), perm)
            step *= 2
    out, at = [], 0
    for p, size in zip(parts, sizes):
        out.append(flat[at : at + size].reshape(p.shape))
        at += size
    return out


def body(
    feats,
    conv_weight,
    conv_bias,
    theta,
    edge_weight,
    inner_edge,
    crossing_segment,
    cut_dest,
    crossing_hyperedge,
    cotangent,
):
    seg = feats.shape[0]
    n_region = lax.axis_size("region")
    n_sub = lax.axis_size("sub")
    device_list = n_region * n_sub
    slot_capacity = max(2, 2 * crossing_segment.shape[0] // device_list)
    slot_total = device_list * slot_capacity
    width = TP * B * C
    def front(rows):
        n = rows.shape[0]
        x4 = rows.reshape(n, T_SIZE, B, C)
        stack = jnp.concatenate([x4[:, k : k + TP] for k in range(KT)], axis=-1)
        u = (
            jnp.einsum("stbk,kf->stbf", stack, conv_weight, preferred_element_type=jnp.float32)
            + conv_bias
        )
        gate = jax.nn.sigmoid(u[..., C:])
        first = u[..., :C]
        hidden = (first * gate).astype(jnp.bfloat16)
        z = (
            jnp.einsum("stbc,cd->stbd", hidden, theta, preferred_element_type=jnp.float32)
            .astype(jnp.bfloat16)
            .reshape(n, width)
        )
        return stack, gate, first, hidden, z

    edge_index = jnp.arange(EDGE_DEV, dtype=jnp.int32)
    incidence = jnp.zeros((EDGE_DEV, seg), jnp.float32)
    for m in range(MEM):
        incidence = incidence + (inner_edge[:, m][None, :] == edge_index[:, None]).astype(
            jnp.float32
        )
    inner_count = jnp.sum(incidence, axis=1)
    incidence = incidence.astype(jnp.bfloat16)
    dest = cut_dest[:, 0]
    dest_hot = (dest[:, None] == jnp.arange(device_list, dtype=jnp.int32)[None, :]).astype(
        jnp.int32
    )
    rank = jnp.sum((jnp.cumsum(dest_hot, axis=0) - 1) * dest_hot, axis=1)
    slot_position = dest * slot_capacity + rank
    slotted_segment = jnp.full((slot_total,), -1, jnp.int32).at[slot_position].set(crossing_segment)
    slotted_hyperedge = (
        jnp.full((slot_total,), -1, jnp.int32).at[slot_position].set(crossing_hyperedge)
    )
    members = (slotted_segment[None, :] == jnp.arange(seg, dtype=jnp.int32)[:, None]).astype(
        jnp.float32
    )
    degree = (MEM + jnp.sum(members, axis=1))[:, None]
    members = members.astype(jnp.bfloat16)
    def pick_slots(rows):
        return jnp.einsum("sn,sf->nf", members, rows, preferred_element_type=jnp.float32).astype(
            jnp.bfloat16
        )

    cut_rows = pick_slots(feats)
    stack, gate, first, hidden, z = front(feats)

    edge_cols = jnp.broadcast_to(slotted_hyperedge.astype(jnp.bfloat16)[:, None], (slot_total, 128))
    in_width = feats.shape[1]
    send = jnp.concatenate([cut_rows, edge_cols], axis=1)
    recv_all = lax.all_to_all(send, ("region", "sub"), split_axis=0, concat_axis=0, tiled=True)
    r_stack, r_gate, r_first, r_hidden, recv = front(recv_all[:, :in_width])
    recv_edge = recv_all[:, in_width].astype(jnp.int32)
    owned = (recv_edge[None, :] == edge_index[:, None]).astype(jnp.float32)
    count = 1.0 + inner_count + jnp.sum(owned, axis=1)
    owned = owned.astype(jnp.bfloat16)
    scale = (edge_weight / count)[:, None]

    def edge_side(local_rows, arrived):
        local, arrived = lax.optimization_barrier(
            (jnp.dot(incidence, local_rows, preferred_element_type=jnp.float32), arrived)
        )
        total = local + jnp.dot(owned, arrived, preferred_element_type=jnp.float32)
        values = (scale * total).astype(jnp.bfloat16)
        returned = jnp.einsum(
            "en,ef->nf", owned, values, preferred_element_type=jnp.float32
        ).astype(jnp.bfloat16)
        return (values, returned)

    def member_side(values, back):
        local, back = lax.optimization_barrier(
            (jnp.einsum("es,ef->sf", incidence, values, preferred_element_type=jnp.float32), back)
        )
        return local + jnp.dot(members, back, preferred_element_type=jnp.float32)

    edge_val, ret_rows = edge_side(z, recv)
    back = lax.all_to_all(ret_rows, ("region", "sub"), split_axis=0, concat_axis=0, tiled=True)
    y = member_side(edge_val, back) / degree
    sig_y = jax.nn.sigmoid(y)
    block_out = (y * sig_y).astype(jnp.bfloat16)
    dy = cotangent.astype(jnp.float32) * sig_y * (1.0 + y * (1.0 - sig_y))
    grad_rows = (dy / degree).astype(jnp.bfloat16)
    send_grads = pick_slots(grad_rows)
    recv_grads = lax.all_to_all(
        send_grads, ("region", "sub"), split_axis=0, concat_axis=0, tiled=True
    )
    dedge, ret_grads = edge_side(grad_rows, recv_grads)
    inner_sum = jnp.einsum("es,ef->sf", incidence, dedge, preferred_element_type=jnp.float32)
    inner_sum, ret_grads = lax.optimization_barrier((inner_sum, ret_grads))
    back_grads = lax.all_to_all(
        ret_grads, ("region", "sub"), split_axis=0, concat_axis=0, tiled=True
    )

    def weight_grads(st, gt, fi, hi, dzr):
        g_theta = jnp.einsum("stbc,stbd->cd", hi, dzr, preferred_element_type=jnp.float32)
        dh = jnp.einsum("stbd,cd->stbc", dzr, theta, preferred_element_type=jnp.float32)
        du = jnp.concatenate([dh * gt, dh * fi * gt * (1.0 - gt)], axis=-1).astype(jnp.bfloat16)
        g_conv = jnp.einsum("stbk,stbf->kf", st, du, preferred_element_type=jnp.float32)
        g_bias = jnp.sum(du.astype(jnp.float32), axis=(0, 1, 2))
        return du, g_conv, g_bias, g_theta

    dz_inner = inner_sum.astype(jnp.bfloat16).reshape(seg, TP, B, C)
    _, ga_conv, ga_bias, ga_theta = weight_grads(stack, gate, first, hidden, dz_inner)
    dz_slots = ret_grads.reshape(slot_total, TP, B, C)
    _, gb_conv, gb_bias, gb_theta = weight_grads(r_stack, r_gate, r_first, r_hidden, dz_slots)
    partial = (ga_conv + gb_conv, ga_bias + gb_bias, ga_theta + gb_theta)
    partial, back_grads = lax.optimization_barrier((partial, back_grads))
    sum_conv, sum_bias, sum_theta = device_sum(partial, device_list)
    dz = (
        (inner_sum + jnp.dot(members, back_grads, preferred_element_type=jnp.float32))
        .astype(jnp.bfloat16)
        .reshape(seg, TP, B, C)
    )
    dh = jnp.einsum("stbd,cd->stbc", dz, theta, preferred_element_type=jnp.float32)
    du = jnp.concatenate([dh * gate, dh * first * gate * (1.0 - gate)], axis=-1).astype(
        jnp.bfloat16
    )
    norm = 1.0 / jnp.sqrt(jnp.float32(seg * device_list * TP * B))
    dstack = jnp.einsum("stbf,kf->stbk", du, conv_weight, preferred_element_type=jnp.float32)
    grad_sum = jnp.zeros((seg, T_SIZE, B, C), jnp.float32)
    for k in range(KT):
        grad_sum = grad_sum + jnp.pad(
            dstack[..., k * C : (k + 1) * C], ((0, 0), (k, KT - 1 - k), (0, 0), (0, 0))
        )
    grad_feats = grad_sum.astype(jnp.bfloat16).reshape(seg, T_SIZE * B * C)
    return (block_out, grad_feats, sum_conv * norm, sum_bias * norm, sum_theta * norm)


def solution(mesh):
    in_specs = (
        P(("region", "sub"), None),
        P(),
        P(),
        P(),
        P(("region", "sub")),
        P(("region", "sub"), None),
        P(("region", "sub")),
        P(("region", "sub"), None),
        P(("region", "sub")),
        P(("region", "sub"), None),
    )
    out_specs = (P(("region", "sub"), None), P(("region", "sub"), None), P(), P(), P())
    return jax.shard_map(body, mesh=mesh, in_specs=in_specs, out_specs=out_specs, check_vma=False)
```

```python
import jax
import jax.numpy as jnp
from jax import lax
from jax.sharding import PartitionSpec as P

C = 64
T_SIZE = 12
B = 2
KT = 3
MEM = 2
TP = 10
EDGE_DEV = 128


def device_sum(parts, n):
    sizes = [p.size for p in parts]
    flat = jnp.concatenate([p.reshape(-1) for p in parts])
    if n & (n - 1):
        flat = lax.psum(flat, ("region", "sub"))
    else:
        step = 1
        while step < n:
            perm = [(i, i ^ step) for i in range(n)]
            flat = flat + lax.ppermute(flat, ("region", "sub"), perm)
            step *= 2
    out, at = [], 0
    for p, size in zip(parts, sizes):
        out.append(flat[at : at + size].reshape(p.shape))
        at += size
    return out


def body(
    feats,
    conv_weight,
    conv_bias,
    theta,
    edge_weight,
    inner_edge,
    crossing_segment,
    cut_dest,
    crossing_hyperedge,
    cotangent,
):
    seg = feats.shape[0]
    n_region = lax.axis_size("region")
    n_sub = lax.axis_size("sub")
    device_list = n_region * n_sub
    slot_capacity = max(2, 2 * crossing_segment.shape[0] // device_list)
    slot_total = device_list * slot_capacity
    width = TP * B * C
    def front(rows):
        n = rows.shape[0]
        x4 = rows.reshape(n, T_SIZE, B, C)
        stack = jnp.concatenate([x4[:, k : k + TP] for k in range(KT)], axis=-1)
        u = (
            jnp.einsum("stbk,kf->stbf", stack, conv_weight, preferred_element_type=jnp.float32)
            + conv_bias
        )
        gate = jax.nn.sigmoid(u[..., C:])
        first = u[..., :C]
        hidden = (first * gate).astype(jnp.bfloat16)
        z = (
            jnp.einsum("stbc,cd->stbd", hidden, theta, preferred_element_type=jnp.float32)
            .astype(jnp.bfloat16)
            .reshape(n, width)
        )
        return stack, gate, first, hidden, z

    edge_index = jnp.arange(EDGE_DEV, dtype=jnp.int32)
    incidence = jnp.zeros((EDGE_DEV, seg), jnp.float32)
    for m in range(MEM):
        incidence = incidence + (inner_edge[:, m][None, :] == edge_index[:, None]).astype(
            jnp.float32
        )
    inner_count = jnp.sum(incidence, axis=1)
    incidence = incidence.astype(jnp.bfloat16)
    dest = cut_dest[:, 0]
    dest_hot = (dest[:, None] == jnp.arange(device_list, dtype=jnp.int32)[None, :]).astype(
        jnp.int32
    )
    rank = jnp.sum((jnp.cumsum(dest_hot, axis=0) - 1) * dest_hot, axis=1)
    slot_position = dest * slot_capacity + rank
    slotted_segment = jnp.full((slot_total,), -1, jnp.int32).at[slot_position].set(crossing_segment)
    slotted_hyperedge = (
        jnp.full((slot_total,), -1, jnp.int32).at[slot_position].set(crossing_hyperedge)
    )
    members = (slotted_segment[None, :] == jnp.arange(seg, dtype=jnp.int32)[:, None]).astype(
        jnp.float32
    )
    degree = (MEM + jnp.sum(members, axis=1))[:, None]
    members = members.astype(jnp.bfloat16)
    def pick_slots(rows):
        return jnp.einsum("sn,sf->nf", members, rows, preferred_element_type=jnp.float32).astype(
            jnp.bfloat16
        )

    cut_rows = pick_slots(feats)
    stack, gate, first, hidden, z = front(feats)

    edge_cols = jnp.broadcast_to(slotted_hyperedge.astype(jnp.bfloat16)[:, None], (slot_total, 128))
    in_width = feats.shape[1]
    send = jnp.concatenate([cut_rows, edge_cols], axis=1)
    recv_all = lax.all_to_all(send, ("region", "sub"), split_axis=0, concat_axis=0, tiled=True)
    r_stack, r_gate, r_first, r_hidden, recv = front(recv_all[:, :in_width])
    recv_edge = recv_all[:, in_width].astype(jnp.int32)
    owned = (recv_edge[None, :] == edge_index[:, None]).astype(jnp.float32)
    count = 1.0 + inner_count + jnp.sum(owned, axis=1)
    owned = owned.astype(jnp.bfloat16)
    scale = (edge_weight / count)[:, None]

    def edge_side(local_rows, arrived):
        total = jnp.dot(incidence, local_rows, preferred_element_type=jnp.float32) + jnp.dot(
            owned, arrived, preferred_element_type=jnp.float32
        )
        values = (scale * total).astype(jnp.bfloat16)
        returned = jnp.einsum(
            "en,ef->nf", owned, values, preferred_element_type=jnp.float32
        ).astype(jnp.bfloat16)
        return (values, returned)

    def member_side(values, back):
        return jnp.einsum(
            "es,ef->sf", incidence, values, preferred_element_type=jnp.float32
        ) + jnp.dot(members, back, preferred_element_type=jnp.float32)

    edge_val, ret_rows = edge_side(z, recv)
    back = lax.all_to_all(ret_rows, ("region", "sub"), split_axis=0, concat_axis=0, tiled=True)
    y = member_side(edge_val, back) / degree
    sig_y = jax.nn.sigmoid(y)
    block_out = (y * sig_y).astype(jnp.bfloat16)
    dy = cotangent.astype(jnp.float32) * sig_y * (1.0 + y * (1.0 - sig_y))
    grad_rows = (dy / degree).astype(jnp.bfloat16)
    send_grads = pick_slots(grad_rows)
    recv_grads = lax.all_to_all(
        send_grads, ("region", "sub"), split_axis=0, concat_axis=0, tiled=True
    )
    dedge, ret_grads = edge_side(grad_rows, recv_grads)
    dedge4 = dedge.reshape(EDGE_DEV, TP, B, C)
    inner_sum = jnp.einsum(
        "es,etbd->stbd", incidence, dedge4, preferred_element_type=jnp.float32
    )
    dz_slots = jnp.einsum(
        "en,etbd->ntbd", owned, dedge4, preferred_element_type=jnp.float32
    ).astype(jnp.bfloat16)
    inner_sum, dz_slots, ret_grads = lax.optimization_barrier((inner_sum, dz_slots, ret_grads))
    back_grads = lax.all_to_all(
        ret_grads, ("region", "sub"), split_axis=0, concat_axis=0, tiled=True
    )

    def weight_grads(st, gt, fi, hi, dzr):
        g_theta = jnp.einsum("stbc,stbd->cd", hi, dzr, preferred_element_type=jnp.float32)
        dh = jnp.einsum("stbd,cd->stbc", dzr, theta, preferred_element_type=jnp.float32)
        du = jnp.concatenate([dh * gt, dh * fi * gt * (1.0 - gt)], axis=-1).astype(jnp.bfloat16)
        g_conv = jnp.einsum("stbk,stbf->kf", st, du, preferred_element_type=jnp.float32)
        g_bias = jnp.sum(du.astype(jnp.float32), axis=(0, 1, 2))
        return du, g_conv, g_bias, g_theta

    dz_inner = inner_sum.astype(jnp.bfloat16)
    _, ga_conv, ga_bias, ga_theta = weight_grads(stack, gate, first, hidden, dz_inner)
    _, gb_conv, gb_bias, gb_theta = weight_grads(r_stack, r_gate, r_first, r_hidden, dz_slots)
    partial = (ga_conv + gb_conv, ga_bias + gb_bias, ga_theta + gb_theta)
    partial, back_grads = lax.optimization_barrier((partial, back_grads))
    sum_conv, sum_bias, sum_theta = device_sum(partial, device_list)
    cut_sum = jnp.einsum(
        "sn,ntbd->stbd",
        members,
        back_grads.reshape(slot_total, TP, B, C),
        preferred_element_type=jnp.float32,
    )
    dz = (inner_sum + cut_sum).astype(jnp.bfloat16)
    dh = jnp.einsum("stbd,cd->stbc", dz, theta, preferred_element_type=jnp.float32)
    du = jnp.concatenate([dh * gate, dh * first * gate * (1.0 - gate)], axis=-1).astype(
        jnp.bfloat16
    )
    norm = 1.0 / jnp.sqrt(jnp.float32(seg * device_list * TP * B))
    dstack = jnp.einsum("stbf,kf->stbk", du, conv_weight, preferred_element_type=jnp.float32)
    grad_sum = jnp.zeros((seg, T_SIZE, B, C), jnp.float32)
    for k in range(KT):
        grad_sum = grad_sum + jnp.pad(
            dstack[..., k * C : (k + 1) * C], ((0, 0), (k, KT - 1 - k), (0, 0), (0, 0))
        )
    grad_feats = grad_sum.astype(jnp.bfloat16).reshape(seg, T_SIZE * B * C)
    return (block_out, grad_feats, sum_conv * norm, sum_bias * norm, sum_theta * norm)


def solution(mesh):
    in_specs = (
        P(("region", "sub"), None),
        P(),
        P(),
        P(),
        P(("region", "sub")),
        P(("region", "sub"), None),
        P(("region", "sub")),
        P(("region", "sub"), None),
        P(("region", "sub")),
        P(("region", "sub"), None),
    )
    out_specs = (P(("region", "sub"), None), P(("region", "sub"), None), P(), P(), P())
    return jax.shard_map(body, mesh=mesh, in_specs=in_specs, out_specs=out_specs, check_vma=False)
```

```python
import jax
import jax.numpy as jnp
from jax import lax
from jax.sharding import PartitionSpec as P

C = 64
T_SIZE = 12
B = 2
KT = 3
MEM = 2
TP = 10
EDGE_DEV = 128


def device_sum(parts, n):
    sizes = [p.size for p in parts]
    flat = jnp.concatenate([p.reshape(-1) for p in parts])
    if n & (n - 1):
        flat = lax.psum(flat, ("region", "sub"))
    else:
        step = 1
        while step < n:
            perm = [(i, i ^ step) for i in range(n)]
            flat = flat + lax.ppermute(flat, ("region", "sub"), perm)
            step *= 2
    out, at = [], 0
    for p, size in zip(parts, sizes):
        out.append(flat[at : at + size].reshape(p.shape))
        at += size
    return out


def body(
    feats,
    conv_weight,
    conv_bias,
    theta,
    edge_weight,
    inner_edge,
    crossing_segment,
    cut_dest,
    crossing_hyperedge,
    cotangent,
):
    seg = feats.shape[0]
    n_region = lax.axis_size("region")
    n_sub = lax.axis_size("sub")
    device_list = n_region * n_sub
    slot_capacity = max(2, 2 * crossing_segment.shape[0] // device_list)
    slot_total = device_list * slot_capacity
    width = TP * B * C
    def front(rows):
        n = rows.shape[0]
        x4 = rows.reshape(n, T_SIZE, B, C)
        stack = jnp.concatenate([x4[:, k : k + TP] for k in range(KT)], axis=-1)
        u = (
            jnp.einsum("stbk,kf->stbf", stack, conv_weight, preferred_element_type=jnp.float32)
            + conv_bias
        )
        gate = jax.nn.sigmoid(u[..., C:])
        first = u[..., :C]
        hidden = (first * gate).astype(jnp.bfloat16)
        z = (
            jnp.einsum("stbc,cd->stbd", hidden, theta, preferred_element_type=jnp.float32)
            .astype(jnp.bfloat16)
            .reshape(n, width)
        )
        return stack, gate, first, hidden, z

    edge_index = jnp.arange(EDGE_DEV, dtype=jnp.int32)
    incidence = jnp.zeros((EDGE_DEV, seg), jnp.float32)
    for m in range(MEM):
        incidence = incidence + (inner_edge[:, m][None, :] == edge_index[:, None]).astype(
            jnp.float32
        )
    inner_count = jnp.sum(incidence, axis=1)
    incidence = incidence.astype(jnp.bfloat16)
    dest = cut_dest[:, 0]
    dest_hot = (dest[:, None] == jnp.arange(device_list, dtype=jnp.int32)[None, :]).astype(
        jnp.int32
    )
    rank = jnp.sum((jnp.cumsum(dest_hot, axis=0) - 1) * dest_hot, axis=1)
    slot_position = dest * slot_capacity + rank
    slotted_segment = jnp.full((slot_total,), -1, jnp.int32).at[slot_position].set(crossing_segment)
    slotted_hyperedge = (
        jnp.full((slot_total,), -1, jnp.int32).at[slot_position].set(crossing_hyperedge)
    )
    members = (slotted_segment[None, :] == jnp.arange(seg, dtype=jnp.int32)[:, None]).astype(
        jnp.float32
    )
    degree = (MEM + jnp.sum(members, axis=1))[:, None]
    members = members.astype(jnp.bfloat16)
    def pick_slots(rows):
        return jnp.einsum("sn,sf->nf", members, rows, preferred_element_type=jnp.float32).astype(
            jnp.bfloat16
        )

    cut_rows = pick_slots(feats)
    stack, gate, first, hidden, z = front(feats)

    edge_cols = jnp.broadcast_to(slotted_hyperedge.astype(jnp.bfloat16)[:, None], (slot_total, 128))
    in_width = feats.shape[1]
    send = jnp.concatenate([cut_rows, edge_cols], axis=1)
    recv_all = lax.all_to_all(send, ("region", "sub"), split_axis=0, concat_axis=0, tiled=True)
    r_stack, r_gate, r_first, r_hidden, recv = front(recv_all[:, :in_width])
    recv_edge = recv_all[:, in_width].astype(jnp.int32)
    owned = (recv_edge[None, :] == edge_index[:, None]).astype(jnp.float32)
    count = 1.0 + inner_count + jnp.sum(owned, axis=1)
    owned = owned.astype(jnp.bfloat16)
    scale = (edge_weight / count)[:, None]

    def edge_side(local_rows, arrived):
        total = jnp.dot(incidence, local_rows, preferred_element_type=jnp.float32) + jnp.dot(
            owned, arrived, preferred_element_type=jnp.float32
        )
        values = (scale * total).astype(jnp.bfloat16)
        returned = jnp.einsum(
            "en,ef->nf", owned, values, preferred_element_type=jnp.float32
        ).astype(jnp.bfloat16)
        return (values, returned)

    def member_side(values, back):
        return jnp.einsum(
            "es,ef->sf", incidence, values, preferred_element_type=jnp.float32
        ) + jnp.dot(members, back, preferred_element_type=jnp.float32)

    edge_val, ret_rows = edge_side(z, recv)
    back = lax.all_to_all(ret_rows, ("region", "sub"), split_axis=0, concat_axis=0, tiled=True)
    y = member_side(edge_val, back) / degree
    sig_y = jax.nn.sigmoid(y)
    block_out = (y * sig_y).astype(jnp.bfloat16)
    dy = cotangent.astype(jnp.float32) * sig_y * (1.0 + y * (1.0 - sig_y))
    grad_rows = (dy / degree).astype(jnp.bfloat16)
    send_grads = pick_slots(grad_rows)
    recv_grads = lax.all_to_all(
        send_grads, ("region", "sub"), split_axis=0, concat_axis=0, tiled=True
    )
    dedge, ret_grads = edge_side(grad_rows, recv_grads)
    inner_sum = jnp.einsum("es,ef->sf", incidence, dedge, preferred_element_type=jnp.float32)
    dz_slots = jnp.einsum(
        "en,etbd->ntbd", owned, dedge.reshape(EDGE_DEV, TP, B, C), preferred_element_type=jnp.float32
    ).astype(jnp.bfloat16)
    inner_sum, dz_slots, ret_grads = lax.optimization_barrier((inner_sum, dz_slots, ret_grads))
    back_grads = lax.all_to_all(
        ret_grads, ("region", "sub"), split_axis=0, concat_axis=0, tiled=True
    )

    def weight_grads(st, gt, fi, hi, dzr):
        g_theta = jnp.einsum("stbc,stbd->cd", hi, dzr, preferred_element_type=jnp.float32)
        dh = jnp.einsum("stbd,cd->stbc", dzr, theta, preferred_element_type=jnp.float32)
        du = jnp.concatenate([dh * gt, dh * fi * gt * (1.0 - gt)], axis=-1).astype(jnp.bfloat16)
        g_conv = jnp.einsum("stbk,stbf->kf", st, du, preferred_element_type=jnp.float32)
        g_bias = jnp.sum(du.astype(jnp.float32), axis=(0, 1, 2))
        return du, g_conv, g_bias, g_theta

    dz_inner = inner_sum.astype(jnp.bfloat16).reshape(seg, TP, B, C)
    _, ga_conv, ga_bias, ga_theta = weight_grads(stack, gate, first, hidden, dz_inner)
    _, gb_conv, gb_bias, gb_theta = weight_grads(r_stack, r_gate, r_first, r_hidden, dz_slots)
    partial = (ga_conv + gb_conv, ga_bias + gb_bias, ga_theta + gb_theta)
    partial, back_grads = lax.optimization_barrier((partial, back_grads))
    sum_conv, sum_bias, sum_theta = device_sum(partial, device_list)
    dz = (
        (inner_sum + jnp.dot(members, back_grads, preferred_element_type=jnp.float32))
        .astype(jnp.bfloat16)
        .reshape(seg, TP, B, C)
    )
    dh = jnp.einsum("stbd,cd->stbc", dz, theta, preferred_element_type=jnp.float32)
    du = jnp.concatenate([dh * gate, dh * first * gate * (1.0 - gate)], axis=-1).astype(
        jnp.bfloat16
    )
    norm = 1.0 / jnp.sqrt(jnp.float32(seg * device_list * TP * B))
    dstack = jnp.einsum("stbf,kf->stbk", du, conv_weight, preferred_element_type=jnp.float32)
    grad_sum = jnp.zeros((seg, T_SIZE, B, C), jnp.float32)
    for k in range(KT):
        grad_sum = grad_sum + jnp.pad(
            dstack[..., k * C : (k + 1) * C], ((0, 0), (k, KT - 1 - k), (0, 0), (0, 0))
        )
    grad_feats = grad_sum.astype(jnp.bfloat16).reshape(seg, T_SIZE * B * C)
    return (block_out, grad_feats, sum_conv * norm, sum_bias * norm, sum_theta * norm)


def solution(mesh):
    in_specs = (
        P(("region", "sub"), None),
        P(),
        P(),
        P(),
        P(("region", "sub")),
        P(("region", "sub"), None),
        P(("region", "sub")),
        P(("region", "sub"), None),
        P(("region", "sub")),
        P(("region", "sub"), None),
    )
    out_specs = (P(("region", "sub"), None), P(("region", "sub"), None), P(), P(), P())
    return jax.shard_map(body, mesh=mesh, in_specs=in_specs, out_specs=out_specs, check_vma=False)
```

```python
import jax
import jax.numpy as jnp
from jax import lax
from jax.sharding import PartitionSpec as P

C = 64
T_SIZE = 12
B = 2
KT = 3
MEM = 2
TP = 10
EDGE_DEV = 128


def device_sum(parts, n):
    sizes = [p.size for p in parts]
    flat = jnp.concatenate([p.reshape(-1) for p in parts])
    if n & (n - 1):
        flat = lax.psum(flat, ("region", "sub"))
    else:
        step = 1
        while step < n:
            perm = [(i, i ^ step) for i in range(n)]
            flat = flat + lax.ppermute(flat, ("region", "sub"), perm)
            step *= 2
    out, at = [], 0
    for p, size in zip(parts, sizes):
        out.append(flat[at : at + size].reshape(p.shape))
        at += size
    return out


def body(
    feats,
    conv_weight,
    conv_bias,
    theta,
    edge_weight,
    inner_edge,
    crossing_segment,
    cut_dest,
    crossing_hyperedge,
    cotangent,
):
    seg = feats.shape[0]
    n_region = lax.axis_size("region")
    n_sub = lax.axis_size("sub")
    device_list = n_region * n_sub
    slot_capacity = max(2, 2 * crossing_segment.shape[0] // device_list)
    slot_total = device_list * slot_capacity
    width = TP * B * C
    def front(rows):
        n = rows.shape[0]
        x4 = rows.reshape(n, T_SIZE, B, C)
        stack = jnp.concatenate([x4[:, k : k + TP] for k in range(KT)], axis=-1)
        u = (
            jnp.einsum("stbk,kf->stbf", stack, conv_weight, preferred_element_type=jnp.float32)
            + conv_bias
        )
        gate = jax.nn.sigmoid(u[..., C:])
        first = u[..., :C]
        hidden = (first * gate).astype(jnp.bfloat16)
        z = (
            jnp.einsum("stbc,cd->stbd", hidden, theta, preferred_element_type=jnp.float32)
            .astype(jnp.bfloat16)
            .reshape(n, width)
        )
        return stack, gate, first, hidden, z

    edge_index = jnp.arange(EDGE_DEV, dtype=jnp.int32)
    incidence = jnp.zeros((EDGE_DEV, seg), jnp.float32)
    for m in range(MEM):
        incidence = incidence + (inner_edge[:, m][None, :] == edge_index[:, None]).astype(
            jnp.float32
        )
    inner_count = jnp.sum(incidence, axis=1)
    incidence = incidence.astype(jnp.bfloat16)
    dest = cut_dest[:, 0]
    n_cut = dest.shape[0]
    order = jnp.arange(n_cut, dtype=jnp.int32)
    earlier = (dest[None, :] == dest[:, None]) & (order[None, :] < order[:, None])
    rank = jnp.sum(earlier.astype(jnp.int32), axis=1)
    slot_position = dest * slot_capacity + rank
    slot_hot = (slot_position[:, None] == jnp.arange(slot_total, dtype=jnp.int32)[None, :]).astype(
        jnp.int32
    )
    slotted_segment = jnp.sum(slot_hot * (crossing_segment[:, None] + 1), axis=0) - 1
    slotted_hyperedge = jnp.sum(slot_hot * (crossing_hyperedge[:, None] + 1), axis=0) - 1
    members = (slotted_segment[None, :] == jnp.arange(seg, dtype=jnp.int32)[:, None]).astype(
        jnp.float32
    )
    degree = (MEM + jnp.sum(members, axis=1))[:, None]
    members = members.astype(jnp.bfloat16)
    def pick_slots(rows):
        return jnp.einsum("sn,sf->nf", members, rows, preferred_element_type=jnp.float32).astype(
            jnp.bfloat16
        )

    cut_rows = pick_slots(feats)
    stack, gate, first, hidden, z = front(feats)

    edge_cols = jnp.broadcast_to(slotted_hyperedge.astype(jnp.bfloat16)[:, None], (slot_total, 128))
    in_width = feats.shape[1]
    send = jnp.concatenate([cut_rows, edge_cols], axis=1)
    recv_all = lax.all_to_all(send, ("region", "sub"), split_axis=0, concat_axis=0, tiled=True)
    r_stack, r_gate, r_first, r_hidden, recv = front(recv_all[:, :in_width])
    recv_edge = recv_all[:, in_width].astype(jnp.int32)
    owned = (recv_edge[None, :] == edge_index[:, None]).astype(jnp.float32)
    count = 1.0 + inner_count + jnp.sum(owned, axis=1)
    owned = owned.astype(jnp.bfloat16)
    scale = (edge_weight / count)[:, None]

    def edge_side(local_rows, arrived):
        total = jnp.dot(incidence, local_rows, preferred_element_type=jnp.float32) + jnp.dot(
            owned, arrived, preferred_element_type=jnp.float32
        )
        values = (scale * total).astype(jnp.bfloat16)
        returned = jnp.einsum(
            "en,ef->nf", owned, values, preferred_element_type=jnp.float32
        ).astype(jnp.bfloat16)
        return (values, returned)

    def member_side(values, back):
        return jnp.einsum(
            "es,ef->sf", incidence, values, preferred_element_type=jnp.float32
        ) + jnp.dot(members, back, preferred_element_type=jnp.float32)

    edge_val, ret_rows = edge_side(z, recv)
    back = lax.all_to_all(ret_rows, ("region", "sub"), split_axis=0, concat_axis=0, tiled=True)
    y = member_side(edge_val, back) / degree
    sig_y = jax.nn.sigmoid(y)
    block_out = (y * sig_y).astype(jnp.bfloat16)
    dy = cotangent.astype(jnp.float32) * sig_y * (1.0 + y * (1.0 - sig_y))
    grad_rows = (dy / degree).astype(jnp.bfloat16)
    send_grads = pick_slots(grad_rows)
    recv_grads = lax.all_to_all(
        send_grads, ("region", "sub"), split_axis=0, concat_axis=0, tiled=True
    )
    dedge, ret_grads = edge_side(grad_rows, recv_grads)
    inner_sum = jnp.einsum("es,ef->sf", incidence, dedge, preferred_element_type=jnp.float32)
    dz_slots = jnp.einsum(
        "en,etbd->ntbd", owned, dedge.reshape(EDGE_DEV, TP, B, C), preferred_element_type=jnp.float32
    ).astype(jnp.bfloat16)
    inner_sum, dz_slots, ret_grads = lax.optimization_barrier((inner_sum, dz_slots, ret_grads))
    back_grads = lax.all_to_all(
        ret_grads, ("region", "sub"), split_axis=0, concat_axis=0, tiled=True
    )

    def weight_grads(st, gt, fi, hi, dzr):
        g_theta = jnp.einsum("stbc,stbd->cd", hi, dzr, preferred_element_type=jnp.float32)
        dh = jnp.einsum("stbd,cd->stbc", dzr, theta, preferred_element_type=jnp.float32)
        du = jnp.concatenate([dh * gt, dh * fi * gt * (1.0 - gt)], axis=-1).astype(jnp.bfloat16)
        g_conv = jnp.einsum("stbk,stbf->kf", st, du, preferred_element_type=jnp.float32)
        g_bias = jnp.sum(du.astype(jnp.float32), axis=(0, 1, 2))
        return du, g_conv, g_bias, g_theta

    dz_inner = inner_sum.astype(jnp.bfloat16).reshape(seg, TP, B, C)
    _, ga_conv, ga_bias, ga_theta = weight_grads(stack, gate, first, hidden, dz_inner)
    _, gb_conv, gb_bias, gb_theta = weight_grads(r_stack, r_gate, r_first, r_hidden, dz_slots)
    partial = (ga_conv + gb_conv, ga_bias + gb_bias, ga_theta + gb_theta)
    partial, back_grads = lax.optimization_barrier((partial, back_grads))
    sum_conv, sum_bias, sum_theta = device_sum(partial, device_list)
    dz = (
        (inner_sum + jnp.dot(members, back_grads, preferred_element_type=jnp.float32))
        .astype(jnp.bfloat16)
        .reshape(seg, TP, B, C)
    )
    dh = jnp.einsum("stbd,cd->stbc", dz, theta, preferred_element_type=jnp.float32)
    du = jnp.concatenate([dh * gate, dh * first * gate * (1.0 - gate)], axis=-1).astype(
        jnp.bfloat16
    )
    norm = 1.0 / jnp.sqrt(jnp.float32(seg * device_list * TP * B))
    dstack = jnp.einsum("stbf,kf->stbk", du, conv_weight, preferred_element_type=jnp.float32)
    grad_sum = jnp.zeros((seg, T_SIZE, B, C), jnp.float32)
    for k in range(KT):
        grad_sum = grad_sum + jnp.pad(
            dstack[..., k * C : (k + 1) * C], ((0, 0), (k, KT - 1 - k), (0, 0), (0, 0))
        )
    grad_feats = grad_sum.astype(jnp.bfloat16).reshape(seg, T_SIZE * B * C)
    return (block_out, grad_feats, sum_conv * norm, sum_bias * norm, sum_theta * norm)


def solution(mesh):
    in_specs = (
        P(("region", "sub"), None),
        P(),
        P(),
        P(),
        P(("region", "sub")),
        P(("region", "sub"), None),
        P(("region", "sub")),
        P(("region", "sub"), None),
        P(("region", "sub")),
        P(("region", "sub"), None),
    )
    out_specs = (P(("region", "sub"), None), P(("region", "sub"), None), P(), P(), P())
    return jax.shard_map(body, mesh=mesh, in_specs=in_specs, out_specs=out_specs, check_vma=False)
```

```python
import jax
import jax.numpy as jnp
from jax import lax
from jax.sharding import PartitionSpec as P

C = 64
T_SIZE = 12
B = 2
KT = 3
MEM = 2
TP = 10
EDGE_DEV = 128


def device_sum(parts, n):
    sizes = [p.size for p in parts]
    flat = jnp.concatenate([p.reshape(-1) for p in parts])
    if n & (n - 1):
        flat = lax.psum(flat, ("region", "sub"))
    else:
        step = 1
        while step < n:
            perm = [(i, i ^ step) for i in range(n)]
            flat = flat + lax.ppermute(flat, ("region", "sub"), perm)
            step *= 2
    out, at = [], 0
    for p, size in zip(parts, sizes):
        out.append(flat[at : at + size].reshape(p.shape))
        at += size
    return out


def body(
    feats,
    conv_weight,
    conv_bias,
    theta,
    edge_weight,
    inner_edge,
    crossing_segment,
    cut_dest,
    crossing_hyperedge,
    cotangent,
):
    seg = feats.shape[0]
    n_region = lax.axis_size("region")
    n_sub = lax.axis_size("sub")
    device_list = n_region * n_sub
    slot_capacity = max(2, 2 * crossing_segment.shape[0] // device_list)
    slot_total = device_list * slot_capacity
    width = TP * B * C
    def front(rows):
        n = rows.shape[0]
        x4 = rows.reshape(n, T_SIZE, B, C)
        stack = jnp.concatenate([x4[:, k : k + TP] for k in range(KT)], axis=-1)
        u = (
            jnp.einsum("stbk,kf->stbf", stack, conv_weight, preferred_element_type=jnp.float32)
            + conv_bias
        )
        gate = jax.nn.sigmoid(u[..., C:])
        first = u[..., :C]
        hidden = (first * gate).astype(jnp.bfloat16)
        z = (
            jnp.einsum("stbc,cd->stbd", hidden, theta, preferred_element_type=jnp.float32)
            .astype(jnp.bfloat16)
            .reshape(n, width)
        )
        return stack, gate, first, hidden, z

    edge_index = jnp.arange(EDGE_DEV, dtype=jnp.int32)
    incidence = jnp.zeros((EDGE_DEV, seg), jnp.float32)
    for m in range(MEM):
        incidence = incidence + (inner_edge[:, m][None, :] == edge_index[:, None]).astype(
            jnp.float32
        )
    inner_count = jnp.sum(incidence, axis=1)
    incidence = incidence.astype(jnp.bfloat16)
    dest = cut_dest[:, 0]
    n_cut = dest.shape[0]
    order = jnp.arange(n_cut, dtype=jnp.int32)
    earlier = (dest[None, :] == dest[:, None]) & (order[None, :] < order[:, None])
    rank = jnp.sum(earlier.astype(jnp.int32), axis=1)
    slot_position = dest * slot_capacity + rank
    slot_hot = (slot_position[:, None] == jnp.arange(slot_total, dtype=jnp.int32)[None, :]).astype(
        jnp.int32
    )
    slotted_segment = jnp.sum(slot_hot * (crossing_segment[:, None] + 1), axis=0) - 1
    slotted_hyperedge = jnp.sum(slot_hot * (crossing_hyperedge[:, None] + 1), axis=0) - 1
    members = (slotted_segment[None, :] == jnp.arange(seg, dtype=jnp.int32)[:, None]).astype(
        jnp.float32
    )
    degree = (MEM + jnp.sum(members, axis=1))[:, None]
    members = members.astype(jnp.bfloat16)
    valid = (slotted_segment >= 0)[:, None]
    slot_deg = jnp.where(
        valid, jnp.einsum("sn,sk->nk", members, degree.astype(jnp.bfloat16), preferred_element_type=jnp.float32), 1.0
    )
    slot_inner = jnp.einsum(
        "es,sn->ne", incidence, members, preferred_element_type=jnp.float32
    ).astype(jnp.bfloat16)
    slot_same = jnp.einsum(
        "sn,sm->nm", members, members, preferred_element_type=jnp.float32
    ).astype(jnp.bfloat16)
    def pick_slots(rows):
        return jnp.einsum("sn,sf->nf", members, rows, preferred_element_type=jnp.float32).astype(
            jnp.bfloat16
        )

    cut_rows = pick_slots(feats)
    stack, gate, first, hidden, z = front(feats)

    edge_cols = jnp.broadcast_to(slotted_hyperedge.astype(jnp.bfloat16)[:, None], (slot_total, 128))
    in_width = feats.shape[1]
    send = jnp.concatenate([cut_rows, edge_cols], axis=1)
    recv_all = lax.all_to_all(send, ("region", "sub"), split_axis=0, concat_axis=0, tiled=True)
    r_stack, r_gate, r_first, r_hidden, recv = front(recv_all[:, :in_width])
    recv_edge = recv_all[:, in_width].astype(jnp.int32)
    owned = (recv_edge[None, :] == edge_index[:, None]).astype(jnp.float32)
    count = 1.0 + inner_count + jnp.sum(owned, axis=1)
    owned = owned.astype(jnp.bfloat16)
    scale = (edge_weight / count)[:, None]

    def edge_side(local_rows, arrived):
        total = jnp.dot(incidence, local_rows, preferred_element_type=jnp.float32) + jnp.dot(
            owned, arrived, preferred_element_type=jnp.float32
        )
        values = (scale * total).astype(jnp.bfloat16)
        returned = jnp.einsum(
            "en,ef->nf", owned, values, preferred_element_type=jnp.float32
        ).astype(jnp.bfloat16)
        return (values, returned)

    def member_side(values, back):
        return jnp.einsum(
            "es,ef->sf", incidence, values, preferred_element_type=jnp.float32
        ) + jnp.dot(members, back, preferred_element_type=jnp.float32)

    edge_val, ret_rows = edge_side(z, recv)
    back = lax.all_to_all(ret_rows, ("region", "sub"), split_axis=0, concat_axis=0, tiled=True)
    y = member_side(edge_val, back) / degree
    sig_y = jax.nn.sigmoid(y)
    block_out = (y * sig_y).astype(jnp.bfloat16)
    dy = cotangent.astype(jnp.float32) * sig_y * (1.0 + y * (1.0 - sig_y))
    grad_rows = (dy / degree).astype(jnp.bfloat16)
    slot_y = (
        jnp.dot(slot_inner, edge_val, preferred_element_type=jnp.float32)
        + jnp.dot(slot_same, back, preferred_element_type=jnp.float32)
    ) / slot_deg
    slot_sig = jax.nn.sigmoid(slot_y)
    slot_dy = pick_slots(cotangent).astype(jnp.float32) * slot_sig * (
        1.0 + slot_y * (1.0 - slot_sig)
    )
    send_grads = (slot_dy / slot_deg).astype(jnp.bfloat16)
    recv_grads = lax.all_to_all(
        send_grads, ("region", "sub"), split_axis=0, concat_axis=0, tiled=True
    )
    dedge, ret_grads = edge_side(grad_rows, recv_grads)
    inner_sum = jnp.einsum("es,ef->sf", incidence, dedge, preferred_element_type=jnp.float32)
    dz_slots = jnp.einsum(
        "en,etbd->ntbd", owned, dedge.reshape(EDGE_DEV, TP, B, C), preferred_element_type=jnp.float32
    ).astype(jnp.bfloat16)
    inner_sum, dz_slots, ret_grads = lax.optimization_barrier((inner_sum, dz_slots, ret_grads))
    back_grads = lax.all_to_all(
        ret_grads, ("region", "sub"), split_axis=0, concat_axis=0, tiled=True
    )

    def weight_grads(st, gt, fi, hi, dzr):
        g_theta = jnp.einsum("stbc,stbd->cd", hi, dzr, preferred_element_type=jnp.float32)
        dh = jnp.einsum("stbd,cd->stbc", dzr, theta, preferred_element_type=jnp.float32)
        du = jnp.concatenate([dh * gt, dh * fi * gt * (1.0 - gt)], axis=-1).astype(jnp.bfloat16)
        g_conv = jnp.einsum("stbk,stbf->kf", st, du, preferred_element_type=jnp.float32)
        g_bias = jnp.sum(du.astype(jnp.float32), axis=(0, 1, 2))
        return du, g_conv, g_bias, g_theta

    dz_inner = inner_sum.astype(jnp.bfloat16).reshape(seg, TP, B, C)
    _, ga_conv, ga_bias, ga_theta = weight_grads(stack, gate, first, hidden, dz_inner)
    _, gb_conv, gb_bias, gb_theta = weight_grads(r_stack, r_gate, r_first, r_hidden, dz_slots)
    partial = (ga_conv + gb_conv, ga_bias + gb_bias, ga_theta + gb_theta)
    partial, back_grads = lax.optimization_barrier((partial, back_grads))
    sum_conv, sum_bias, sum_theta = device_sum(partial, device_list)
    dz = (
        (inner_sum + jnp.dot(members, back_grads, preferred_element_type=jnp.float32))
        .astype(jnp.bfloat16)
        .reshape(seg, TP, B, C)
    )
    dh = jnp.einsum("stbd,cd->stbc", dz, theta, preferred_element_type=jnp.float32)
    du = jnp.concatenate([dh * gate, dh * first * gate * (1.0 - gate)], axis=-1).astype(
        jnp.bfloat16
    )
    norm = 1.0 / jnp.sqrt(jnp.float32(seg * device_list * TP * B))
    dstack = jnp.einsum("stbf,kf->stbk", du, conv_weight, preferred_element_type=jnp.float32)
    grad_sum = jnp.zeros((seg, T_SIZE, B, C), jnp.float32)
    for k in range(KT):
        grad_sum = grad_sum + jnp.pad(
            dstack[..., k * C : (k + 1) * C], ((0, 0), (k, KT - 1 - k), (0, 0), (0, 0))
        )
    grad_feats = grad_sum.astype(jnp.bfloat16).reshape(seg, T_SIZE * B * C)
    return (block_out, grad_feats, sum_conv * norm, sum_bias * norm, sum_theta * norm)


def solution(mesh):
    in_specs = (
        P(("region", "sub"), None),
        P(),
        P(),
        P(),
        P(("region", "sub")),
        P(("region", "sub"), None),
        P(("region", "sub")),
        P(("region", "sub"), None),
        P(("region", "sub")),
        P(("region", "sub"), None),
    )
    out_specs = (P(("region", "sub"), None), P(("region", "sub"), None), P(), P(), P())
    return jax.shard_map(body, mesh=mesh, in_specs=in_specs, out_specs=out_specs, check_vma=False)
```

```python
import jax
import jax.numpy as jnp
from jax import lax
from jax.sharding import PartitionSpec as P

C = 64
T_SIZE = 12
B = 2
KT = 3
MEM = 2
TP = 10
EDGE_DEV = 128


def device_sum(parts, n):
    sizes = [p.size for p in parts]
    flat = jnp.concatenate([p.reshape(-1) for p in parts])
    if n & (n - 1):
        flat = lax.psum(flat, ("region", "sub"))
    else:
        step = n // 2
        while step >= 1:
            perm = [(i, i ^ step) for i in range(n)]
            flat = flat + lax.ppermute(flat, ("region", "sub"), perm)
            step //= 2
    out, at = [], 0
    for p, size in zip(parts, sizes):
        out.append(flat[at : at + size].reshape(p.shape))
        at += size
    return out


def body(
    feats,
    conv_weight,
    conv_bias,
    theta,
    edge_weight,
    inner_edge,
    crossing_segment,
    cut_dest,
    crossing_hyperedge,
    cotangent,
):
    seg = feats.shape[0]
    n_region = lax.axis_size("region")
    n_sub = lax.axis_size("sub")
    device_list = n_region * n_sub
    slot_capacity = max(2, 2 * crossing_segment.shape[0] // device_list)
    slot_total = device_list * slot_capacity
    width = TP * B * C
    def front(rows):
        n = rows.shape[0]
        x4 = rows.reshape(n, T_SIZE, B, C)
        stack = jnp.concatenate([x4[:, k : k + TP] for k in range(KT)], axis=-1)
        u = (
            jnp.einsum("stbk,kf->stbf", stack, conv_weight, preferred_element_type=jnp.float32)
            + conv_bias
        )
        gate = jax.nn.sigmoid(u[..., C:])
        first = u[..., :C]
        hidden = (first * gate).astype(jnp.bfloat16)
        z = (
            jnp.einsum("stbc,cd->stbd", hidden, theta, preferred_element_type=jnp.float32)
            .astype(jnp.bfloat16)
            .reshape(n, width)
        )
        return stack, gate, first, hidden, z

    edge_index = jnp.arange(EDGE_DEV, dtype=jnp.int32)
    incidence = jnp.zeros((EDGE_DEV, seg), jnp.float32)
    for m in range(MEM):
        incidence = incidence + (inner_edge[:, m][None, :] == edge_index[:, None]).astype(
            jnp.float32
        )
    inner_count = jnp.sum(incidence, axis=1)
    incidence = incidence.astype(jnp.bfloat16)
    dest = cut_dest[:, 0]
    n_cut = dest.shape[0]
    order = jnp.arange(n_cut, dtype=jnp.int32)
    earlier = (dest[None, :] == dest[:, None]) & (order[None, :] < order[:, None])
    rank = jnp.sum(earlier.astype(jnp.int32), axis=1)
    slot_position = dest * slot_capacity + rank
    slot_hot = (slot_position[:, None] == jnp.arange(slot_total, dtype=jnp.int32)[None, :]).astype(
        jnp.int32
    )
    slotted_segment = jnp.sum(slot_hot * (crossing_segment[:, None] + 1), axis=0) - 1
    slotted_hyperedge = jnp.sum(slot_hot * (crossing_hyperedge[:, None] + 1), axis=0) - 1
    members = (slotted_segment[None, :] == jnp.arange(seg, dtype=jnp.int32)[:, None]).astype(
        jnp.float32
    )
    degree = (MEM + jnp.sum(members, axis=1))[:, None]
    members = members.astype(jnp.bfloat16)
    def pick_slots(rows):
        return jnp.einsum("sn,sf->nf", members, rows, preferred_element_type=jnp.float32).astype(
            jnp.bfloat16
        )

    cut_rows = pick_slots(feats)
    stack, gate, first, hidden, z = front(feats)

    edge_cols = jnp.broadcast_to(slotted_hyperedge.astype(jnp.bfloat16)[:, None], (slot_total, 128))
    in_width = feats.shape[1]
    send = jnp.concatenate([cut_rows, edge_cols], axis=1)
    recv_all = lax.all_to_all(send, ("region", "sub"), split_axis=0, concat_axis=0, tiled=True)
    r_stack, r_gate, r_first, r_hidden, recv = front(recv_all[:, :in_width])
    recv_edge = recv_all[:, in_width].astype(jnp.int32)
    owned = (recv_edge[None, :] == edge_index[:, None]).astype(jnp.float32)
    count = 1.0 + inner_count + jnp.sum(owned, axis=1)
    owned = owned.astype(jnp.bfloat16)
    scale = (edge_weight / count)[:, None]

    def edge_side(local_rows, arrived):
        total = jnp.dot(incidence, local_rows, preferred_element_type=jnp.float32) + jnp.dot(
            owned, arrived, preferred_element_type=jnp.float32
        )
        values = (scale * total).astype(jnp.bfloat16)
        returned = jnp.einsum(
            "en,ef->nf", owned, values, preferred_element_type=jnp.float32
        ).astype(jnp.bfloat16)
        return (values, returned)

    def member_side(values, back):
        return jnp.einsum(
            "es,ef->sf", incidence, values, preferred_element_type=jnp.float32
        ) + jnp.dot(members, back, preferred_element_type=jnp.float32)

    edge_val, ret_rows = edge_side(z, recv)
    back = lax.all_to_all(ret_rows, ("region", "sub"), split_axis=0, concat_axis=0, tiled=True)
    y = member_side(edge_val, back) / degree
    sig_y = jax.nn.sigmoid(y)
    block_out = (y * sig_y).astype(jnp.bfloat16)
    dy = cotangent.astype(jnp.float32) * sig_y * (1.0 + y * (1.0 - sig_y))
    grad_rows = (dy / degree).astype(jnp.bfloat16)
    send_grads = pick_slots(grad_rows)
    recv_grads = lax.all_to_all(
        send_grads, ("region", "sub"), split_axis=0, concat_axis=0, tiled=True
    )
    dedge, ret_grads = edge_side(grad_rows, recv_grads)
    inner_sum = jnp.einsum("es,ef->sf", incidence, dedge, preferred_element_type=jnp.float32)
    dz_slots = jnp.einsum(
        "en,etbd->ntbd", owned, dedge.reshape(EDGE_DEV, TP, B, C), preferred_element_type=jnp.float32
    ).astype(jnp.bfloat16)
    inner_sum, dz_slots, ret_grads = lax.optimization_barrier((inner_sum, dz_slots, ret_grads))
    back_grads = lax.all_to_all(
        ret_grads, ("region", "sub"), split_axis=0, concat_axis=0, tiled=True
    )

    def weight_grads(st, gt, fi, hi, dzr):
        g_theta = jnp.einsum("stbc,stbd->cd", hi, dzr, preferred_element_type=jnp.float32)
        dh = jnp.einsum("stbd,cd->stbc", dzr, theta, preferred_element_type=jnp.float32)
        du = jnp.concatenate([dh * gt, dh * fi * gt * (1.0 - gt)], axis=-1).astype(jnp.bfloat16)
        g_conv = jnp.einsum("stbk,stbf->kf", st, du, preferred_element_type=jnp.float32)
        g_bias = jnp.sum(du.astype(jnp.float32), axis=(0, 1, 2))
        return du, g_conv, g_bias, g_theta

    dz_inner = inner_sum.astype(jnp.bfloat16).reshape(seg, TP, B, C)
    _, ga_conv, ga_bias, ga_theta = weight_grads(stack, gate, first, hidden, dz_inner)
    _, gb_conv, gb_bias, gb_theta = weight_grads(r_stack, r_gate, r_first, r_hidden, dz_slots)
    partial = (ga_conv + gb_conv, ga_bias + gb_bias, ga_theta + gb_theta)
    partial, back_grads = lax.optimization_barrier((partial, back_grads))
    sum_conv, sum_bias, sum_theta = device_sum(partial, device_list)
    dz = (
        (inner_sum + jnp.dot(members, back_grads, preferred_element_type=jnp.float32))
        .astype(jnp.bfloat16)
        .reshape(seg, TP, B, C)
    )
    dh = jnp.einsum("stbd,cd->stbc", dz, theta, preferred_element_type=jnp.float32)
    du = jnp.concatenate([dh * gate, dh * first * gate * (1.0 - gate)], axis=-1).astype(
        jnp.bfloat16
    )
    norm = 1.0 / jnp.sqrt(jnp.float32(seg * device_list * TP * B))
    dstack = jnp.einsum("stbf,kf->stbk", du, conv_weight, preferred_element_type=jnp.float32)
    grad_sum = jnp.zeros((seg, T_SIZE, B, C), jnp.float32)
    for k in range(KT):
        grad_sum = grad_sum + jnp.pad(
            dstack[..., k * C : (k + 1) * C], ((0, 0), (k, KT - 1 - k), (0, 0), (0, 0))
        )
    grad_feats = grad_sum.astype(jnp.bfloat16).reshape(seg, T_SIZE * B * C)
    return (block_out, grad_feats, sum_conv * norm, sum_bias * norm, sum_theta * norm)


def solution(mesh):
    in_specs = (
        P(("region", "sub"), None),
        P(),
        P(),
        P(),
        P(("region", "sub")),
        P(("region", "sub"), None),
        P(("region", "sub")),
        P(("region", "sub"), None),
        P(("region", "sub")),
        P(("region", "sub"), None),
    )
    out_specs = (P(("region", "sub"), None), P(("region", "sub"), None), P(), P(), P())
    return jax.shard_map(body, mesh=mesh, in_specs=in_specs, out_specs=out_specs, check_vma=False)
```

```python
import jax
import jax.numpy as jnp
from jax import lax
from jax.sharding import PartitionSpec as P

C = 64
T_SIZE = 12
B = 2
KT = 3
MEM = 2
TP = 10
EDGE_DEV = 128


def device_sum(parts, n):
    sizes = [p.size for p in parts]
    flat = jnp.concatenate([p.reshape(-1) for p in parts])
    if n & (n - 1):
        flat = lax.psum(flat, ("region", "sub"))
    else:
        step = 1
        while step < n:
            perm = [(i, i ^ step) for i in range(n)]
            flat = flat + lax.ppermute(flat, ("region", "sub"), perm)
            step *= 2
    out, at = [], 0
    for p, size in zip(parts, sizes):
        out.append(flat[at : at + size].reshape(p.shape))
        at += size
    return out


def body(
    feats,
    conv_weight,
    conv_bias,
    theta,
    edge_weight,
    inner_edge,
    crossing_segment,
    cut_dest,
    crossing_hyperedge,
    cotangent,
):
    seg = feats.shape[0]
    n_region = lax.axis_size("region")
    n_sub = lax.axis_size("sub")
    device_list = n_region * n_sub
    slot_capacity = max(2, 2 * crossing_segment.shape[0] // device_list)
    slot_total = device_list * slot_capacity
    width = TP * B * C
    def front(rows):
        n = rows.shape[0]
        x4 = rows.reshape(n, T_SIZE, B, C)
        stack = jnp.concatenate([x4[:, k : k + TP] for k in range(KT)], axis=-1)
        u = (
            jnp.einsum("stbk,kf->stbf", stack, conv_weight, preferred_element_type=jnp.float32)
            + conv_bias
        )
        gate = jax.nn.sigmoid(u[..., C:])
        first = u[..., :C]
        hidden = (first * gate).astype(jnp.bfloat16)
        z = (
            jnp.einsum("stbc,cd->stbd", hidden, theta, preferred_element_type=jnp.float32)
            .astype(jnp.bfloat16)
            .reshape(n, width)
        )
        return stack, gate, first, hidden, z

    edge_index = jnp.arange(EDGE_DEV, dtype=jnp.int32)
    incidence = jnp.zeros((EDGE_DEV, seg), jnp.float32)
    for m in range(MEM):
        incidence = incidence + (inner_edge[:, m][None, :] == edge_index[:, None]).astype(
            jnp.float32
        )
    inner_count = jnp.sum(incidence, axis=1)
    incidence = incidence.astype(jnp.bfloat16)
    dest = cut_dest[:, 0]
    n_cut = dest.shape[0]
    order = jnp.arange(n_cut, dtype=jnp.int32)
    earlier = (dest[None, :] == dest[:, None]) & (order[None, :] < order[:, None])
    rank = jnp.sum(earlier.astype(jnp.int32), axis=1)
    slot_position = dest * slot_capacity + rank
    slot_hot = (slot_position[:, None] == jnp.arange(slot_total, dtype=jnp.int32)[None, :]).astype(
        jnp.int32
    )
    slotted_segment = jnp.sum(slot_hot * (crossing_segment[:, None] + 1), axis=0) - 1
    slotted_hyperedge = jnp.sum(slot_hot * (crossing_hyperedge[:, None] + 1), axis=0) - 1
    members = (slotted_segment[None, :] == jnp.arange(seg, dtype=jnp.int32)[:, None]).astype(
        jnp.float32
    )
    degree = (MEM + jnp.sum(members, axis=1))[:, None]
    members = members.astype(jnp.bfloat16)
    def pick_slots(rows):
        return jnp.einsum("sn,sf->nf", members, rows, preferred_element_type=jnp.float32).astype(
            jnp.bfloat16
        )

    cut_rows = pick_slots(feats)
    stack, gate, first, hidden, z = front(feats)

    def gate_factors(gt, fi):
        return lax.optimization_barrier(
            ((gt).astype(jnp.bfloat16), (fi * gt * (1.0 - gt)).astype(jnp.bfloat16))
        )

    fa, fb = gate_factors(gate, first)

    edge_cols = jnp.broadcast_to(slotted_hyperedge.astype(jnp.bfloat16)[:, None], (slot_total, 128))
    in_width = feats.shape[1]
    send = jnp.concatenate([cut_rows, edge_cols], axis=1)
    recv_all = lax.all_to_all(send, ("region", "sub"), split_axis=0, concat_axis=0, tiled=True)
    r_stack, r_gate, r_first, r_hidden, recv = front(recv_all[:, :in_width])
    r_fa, r_fb = gate_factors(r_gate, r_first)
    recv_edge = recv_all[:, in_width].astype(jnp.int32)
    owned = (recv_edge[None, :] == edge_index[:, None]).astype(jnp.float32)
    count = 1.0 + inner_count + jnp.sum(owned, axis=1)
    owned = owned.astype(jnp.bfloat16)
    scale = (edge_weight / count)[:, None]

    def edge_side(local_rows, arrived):
        total = jnp.dot(incidence, local_rows, preferred_element_type=jnp.float32) + jnp.dot(
            owned, arrived, preferred_element_type=jnp.float32
        )
        values = (scale * total).astype(jnp.bfloat16)
        returned = jnp.einsum(
            "en,ef->nf", owned, values, preferred_element_type=jnp.float32
        ).astype(jnp.bfloat16)
        return (values, returned)

    def member_side(values, back):
        return jnp.einsum(
            "es,ef->sf", incidence, values, preferred_element_type=jnp.float32
        ) + jnp.dot(members, back, preferred_element_type=jnp.float32)

    edge_val, ret_rows = edge_side(z, recv)
    back = lax.all_to_all(ret_rows, ("region", "sub"), split_axis=0, concat_axis=0, tiled=True)
    y = member_side(edge_val, back) / degree
    sig_y = jax.nn.sigmoid(y)
    block_out = (y * sig_y).astype(jnp.bfloat16)
    dy = cotangent.astype(jnp.float32) * sig_y * (1.0 + y * (1.0 - sig_y))
    grad_rows = (dy / degree).astype(jnp.bfloat16)
    send_grads = pick_slots(grad_rows)
    recv_grads = lax.all_to_all(
        send_grads, ("region", "sub"), split_axis=0, concat_axis=0, tiled=True
    )
    dedge, ret_grads = edge_side(grad_rows, recv_grads)
    inner_sum = jnp.einsum("es,ef->sf", incidence, dedge, preferred_element_type=jnp.float32)
    dz_slots = jnp.einsum(
        "en,etbd->ntbd", owned, dedge.reshape(EDGE_DEV, TP, B, C), preferred_element_type=jnp.float32
    ).astype(jnp.bfloat16)
    inner_sum, dz_slots, ret_grads = lax.optimization_barrier((inner_sum, dz_slots, ret_grads))
    back_grads = lax.all_to_all(
        ret_grads, ("region", "sub"), split_axis=0, concat_axis=0, tiled=True
    )

    def weight_grads(st, gt, fi, hi, dzr):
        g_theta = jnp.einsum("stbc,stbd->cd", hi, dzr, preferred_element_type=jnp.float32)
        dh = jnp.einsum("stbd,cd->stbc", dzr, theta, preferred_element_type=jnp.float32)
        du = jnp.concatenate([dh * gt, dh * fi], axis=-1).astype(jnp.bfloat16)
        g_conv = jnp.einsum("stbk,stbf->kf", st, du, preferred_element_type=jnp.float32)
        g_bias = jnp.sum(du.astype(jnp.float32), axis=(0, 1, 2))
        return du, g_conv, g_bias, g_theta

    dz_inner = inner_sum.astype(jnp.bfloat16).reshape(seg, TP, B, C)
    _, ga_conv, ga_bias, ga_theta = weight_grads(stack, fa, fb, hidden, dz_inner)
    _, gb_conv, gb_bias, gb_theta = weight_grads(r_stack, r_fa, r_fb, r_hidden, dz_slots)
    partial = (ga_conv + gb_conv, ga_bias + gb_bias, ga_theta + gb_theta)
    partial, back_grads = lax.optimization_barrier((partial, back_grads))
    sum_conv, sum_bias, sum_theta = device_sum(partial, device_list)
    dz = (
        (inner_sum + jnp.dot(members, back_grads, preferred_element_type=jnp.float32))
        .astype(jnp.bfloat16)
        .reshape(seg, TP, B, C)
    )
    dh = jnp.einsum("stbd,cd->stbc", dz, theta, preferred_element_type=jnp.float32)
    du = jnp.concatenate([dh * fa, dh * fb], axis=-1).astype(
        jnp.bfloat16
    )
    norm = 1.0 / jnp.sqrt(jnp.float32(seg * device_list * TP * B))
    dstack = jnp.einsum("stbf,kf->stbk", du, conv_weight, preferred_element_type=jnp.float32)
    grad_sum = jnp.zeros((seg, T_SIZE, B, C), jnp.float32)
    for k in range(KT):
        grad_sum = grad_sum + jnp.pad(
            dstack[..., k * C : (k + 1) * C], ((0, 0), (k, KT - 1 - k), (0, 0), (0, 0))
        )
    grad_feats = grad_sum.astype(jnp.bfloat16).reshape(seg, T_SIZE * B * C)
    return (block_out, grad_feats, sum_conv * norm, sum_bias * norm, sum_theta * norm)


def solution(mesh):
    in_specs = (
        P(("region", "sub"), None),
        P(),
        P(),
        P(),
        P(("region", "sub")),
        P(("region", "sub"), None),
        P(("region", "sub")),
        P(("region", "sub"), None),
        P(("region", "sub")),
        P(("region", "sub"), None),
    )
    out_specs = (P(("region", "sub"), None), P(("region", "sub"), None), P(), P(), P())
    return jax.shard_map(body, mesh=mesh, in_specs=in_specs, out_specs=out_specs, check_vma=False)
```

```python
import jax
import jax.numpy as jnp
from jax import lax
from jax.sharding import PartitionSpec as P

C = 64
T_SIZE = 12
B = 2
KT = 3
MEM = 2
TP = 10
EDGE_DEV = 128


def device_sum(parts, n, tie):
    sizes = [p.size for p in parts]
    flat = jnp.concatenate([p.reshape(-1) for p in parts])
    if n & (n - 1):
        flat, tie = lax.optimization_barrier((flat, tie))
        flat = lax.psum(flat, ("region", "sub"))
    else:
        step = 1
        while step < n:
            perm = [(i, i ^ step) for i in range(n)]
            flat = flat + lax.ppermute(flat, ("region", "sub"), perm)
            if step == 1:
                flat, tie = lax.optimization_barrier((flat, tie))
            step *= 2
        if n == 1:
            flat, tie = lax.optimization_barrier((flat, tie))
    out, at = [], 0
    for p, size in zip(parts, sizes):
        out.append(flat[at : at + size].reshape(p.shape))
        at += size
    return out, tie


def body(
    feats,
    conv_weight,
    conv_bias,
    theta,
    edge_weight,
    inner_edge,
    crossing_segment,
    cut_dest,
    crossing_hyperedge,
    cotangent,
):
    seg = feats.shape[0]
    n_region = lax.axis_size("region")
    n_sub = lax.axis_size("sub")
    device_list = n_region * n_sub
    slot_capacity = max(2, 2 * crossing_segment.shape[0] // device_list)
    slot_total = device_list * slot_capacity
    width = TP * B * C
    def front(rows):
        n = rows.shape[0]
        x4 = rows.reshape(n, T_SIZE, B, C)
        stack = jnp.concatenate([x4[:, k : k + TP] for k in range(KT)], axis=-1)
        u = (
            jnp.einsum("stbk,kf->stbf", stack, conv_weight, preferred_element_type=jnp.float32)
            + conv_bias
        )
        gate = jax.nn.sigmoid(u[..., C:])
        first = u[..., :C]
        hidden = (first * gate).astype(jnp.bfloat16)
        z = (
            jnp.einsum("stbc,cd->stbd", hidden, theta, preferred_element_type=jnp.float32)
            .astype(jnp.bfloat16)
            .reshape(n, width)
        )
        return stack, gate, first, hidden, z

    edge_index = jnp.arange(EDGE_DEV, dtype=jnp.int32)
    incidence = jnp.zeros((EDGE_DEV, seg), jnp.float32)
    for m in range(MEM):
        incidence = incidence + (inner_edge[:, m][None, :] == edge_index[:, None]).astype(
            jnp.float32
        )
    inner_count = jnp.sum(incidence, axis=1)
    incidence = incidence.astype(jnp.bfloat16)
    dest = cut_dest[:, 0]
    n_cut = dest.shape[0]
    order = jnp.arange(n_cut, dtype=jnp.int32)
    earlier = (dest[None, :] == dest[:, None]) & (order[None, :] < order[:, None])
    rank = jnp.sum(earlier.astype(jnp.int32), axis=1)
    slot_position = dest * slot_capacity + rank
    slot_hot = (slot_position[:, None] == jnp.arange(slot_total, dtype=jnp.int32)[None, :]).astype(
        jnp.int32
    )
    slotted_segment = jnp.sum(slot_hot * (crossing_segment[:, None] + 1), axis=0) - 1
    slotted_hyperedge = jnp.sum(slot_hot * (crossing_hyperedge[:, None] + 1), axis=0) - 1
    members = (slotted_segment[None, :] == jnp.arange(seg, dtype=jnp.int32)[:, None]).astype(
        jnp.float32
    )
    degree = (MEM + jnp.sum(members, axis=1))[:, None]
    members = members.astype(jnp.bfloat16)
    def pick_slots(rows):
        return jnp.einsum("sn,sf->nf", members, rows, preferred_element_type=jnp.float32).astype(
            jnp.bfloat16
        )

    cut_rows = pick_slots(feats)
    stack, gate, first, hidden, z = front(feats)

    edge_cols = jnp.broadcast_to(slotted_hyperedge.astype(jnp.bfloat16)[:, None], (slot_total, 128))
    in_width = feats.shape[1]
    send = jnp.concatenate([cut_rows, edge_cols], axis=1)
    recv_all = lax.all_to_all(send, ("region", "sub"), split_axis=0, concat_axis=0, tiled=True)
    r_stack, r_gate, r_first, r_hidden, recv = front(recv_all[:, :in_width])
    recv_edge = recv_all[:, in_width].astype(jnp.int32)
    owned = (recv_edge[None, :] == edge_index[:, None]).astype(jnp.float32)
    count = 1.0 + inner_count + jnp.sum(owned, axis=1)
    owned = owned.astype(jnp.bfloat16)
    scale = (edge_weight / count)[:, None]

    def edge_side(local_rows, arrived):
        total = jnp.dot(incidence, local_rows, preferred_element_type=jnp.float32) + jnp.dot(
            owned, arrived, preferred_element_type=jnp.float32
        )
        values = (scale * total).astype(jnp.bfloat16)
        returned = jnp.einsum(
            "en,ef->nf", owned, values, preferred_element_type=jnp.float32
        ).astype(jnp.bfloat16)
        return (values, returned)

    def member_side(values, back):
        return jnp.einsum(
            "es,ef->sf", incidence, values, preferred_element_type=jnp.float32
        ) + jnp.dot(members, back, preferred_element_type=jnp.float32)

    edge_val, ret_rows = edge_side(z, recv)
    back = lax.all_to_all(ret_rows, ("region", "sub"), split_axis=0, concat_axis=0, tiled=True)
    y = member_side(edge_val, back) / degree
    sig_y = jax.nn.sigmoid(y)
    block_out = (y * sig_y).astype(jnp.bfloat16)
    dy = cotangent.astype(jnp.float32) * sig_y * (1.0 + y * (1.0 - sig_y))
    grad_rows = (dy / degree).astype(jnp.bfloat16)
    send_grads = pick_slots(grad_rows)
    recv_grads = lax.all_to_all(
        send_grads, ("region", "sub"), split_axis=0, concat_axis=0, tiled=True
    )
    dedge, ret_grads = edge_side(grad_rows, recv_grads)
    inner_sum = jnp.einsum("es,ef->sf", incidence, dedge, preferred_element_type=jnp.float32)
    dz_slots = jnp.einsum(
        "en,etbd->ntbd", owned, dedge.reshape(EDGE_DEV, TP, B, C), preferred_element_type=jnp.float32
    ).astype(jnp.bfloat16)
    inner_sum, dz_slots, ret_grads = lax.optimization_barrier((inner_sum, dz_slots, ret_grads))
    back_grads = lax.all_to_all(
        ret_grads, ("region", "sub"), split_axis=0, concat_axis=0, tiled=True
    )

    def weight_grads(st, gt, fi, hi, dzr):
        g_theta = jnp.einsum("stbc,stbd->cd", hi, dzr, preferred_element_type=jnp.float32)
        dh = jnp.einsum("stbd,cd->stbc", dzr, theta, preferred_element_type=jnp.float32)
        du = jnp.concatenate([dh * gt, dh * fi * gt * (1.0 - gt)], axis=-1).astype(jnp.bfloat16)
        g_conv = jnp.einsum("stbk,stbf->kf", st, du, preferred_element_type=jnp.float32)
        g_bias = jnp.sum(du.astype(jnp.float32), axis=(0, 1, 2))
        return du, g_conv, g_bias, g_theta

    dz_inner = inner_sum.astype(jnp.bfloat16).reshape(seg, TP, B, C)
    _, ga_conv, ga_bias, ga_theta = weight_grads(stack, gate, first, hidden, dz_inner)
    _, gb_conv, gb_bias, gb_theta = weight_grads(r_stack, r_gate, r_first, r_hidden, dz_slots)
    partial = (ga_conv + gb_conv, ga_bias + gb_bias, ga_theta + gb_theta)
    (sum_conv, sum_bias, sum_theta), back_grads = device_sum(partial, device_list, back_grads)
    dz = (
        (inner_sum + jnp.dot(members, back_grads, preferred_element_type=jnp.float32))
        .astype(jnp.bfloat16)
        .reshape(seg, TP, B, C)
    )
    dh = jnp.einsum("stbd,cd->stbc", dz, theta, preferred_element_type=jnp.float32)
    du = jnp.concatenate([dh * gate, dh * first * gate * (1.0 - gate)], axis=-1).astype(
        jnp.bfloat16
    )
    norm = 1.0 / jnp.sqrt(jnp.float32(seg * device_list * TP * B))
    dstack = jnp.einsum("stbf,kf->stbk", du, conv_weight, preferred_element_type=jnp.float32)
    grad_sum = jnp.zeros((seg, T_SIZE, B, C), jnp.float32)
    for k in range(KT):
        grad_sum = grad_sum + jnp.pad(
            dstack[..., k * C : (k + 1) * C], ((0, 0), (k, KT - 1 - k), (0, 0), (0, 0))
        )
    grad_feats = grad_sum.astype(jnp.bfloat16).reshape(seg, T_SIZE * B * C)
    return (block_out, grad_feats, sum_conv * norm, sum_bias * norm, sum_theta * norm)


def solution(mesh):
    in_specs = (
        P(("region", "sub"), None),
        P(),
        P(),
        P(),
        P(("region", "sub")),
        P(("region", "sub"), None),
        P(("region", "sub")),
        P(("region", "sub"), None),
        P(("region", "sub")),
        P(("region", "sub"), None),
    )
    out_specs = (P(("region", "sub"), None), P(("region", "sub"), None), P(), P(), P())
    return jax.shard_map(body, mesh=mesh, in_specs=in_specs, out_specs=out_specs, check_vma=False)
```

```python
import jax
import jax.numpy as jnp
from jax import lax
from jax.sharding import PartitionSpec as P

C = 64
T_SIZE = 12
B = 2
KT = 3
MEM = 2
TP = 10
EDGE_DEV = 128


def device_sum(parts, n, tie):
    sizes = [p.size for p in parts]
    flat = jnp.concatenate([p.reshape(-1) for p in parts])
    if n & (n - 1):
        flat, tie = lax.optimization_barrier((flat, tie))
        flat = lax.psum(flat, ("region", "sub"))
    else:
        axes = ("region", "sub")
        if n == 1 or flat.shape[0] % 2:
            flat, tie = lax.optimization_barrier((flat, tie))
            step = 1
            while step < n:
                flat = flat + lax.ppermute(flat, axes, [(i, i ^ step) for i in range(n)])
                step *= 2
        else:
            half = flat.shape[0] // 2
            low = lax.axis_index(axes) % 2 == 0
            lo, hi = flat[:half], flat[half:]
            pair = [(i, i ^ 1) for i in range(n)]
            kept = jnp.where(low, lo, hi) + lax.ppermute(jnp.where(low, hi, lo), axes, pair)
            kept, tie = lax.optimization_barrier((kept, tie))
            step = 2
            while step < n:
                kept = kept + lax.ppermute(kept, axes, [(i, i ^ step) for i in range(n)])
                step *= 2
            other = lax.ppermute(kept, axes, pair)
            flat = jnp.where(
                low, jnp.concatenate([kept, other]), jnp.concatenate([other, kept])
            )
    out, at = [], 0
    for p, size in zip(parts, sizes):
        out.append(flat[at : at + size].reshape(p.shape))
        at += size
    return out, tie


def body(
    feats,
    conv_weight,
    conv_bias,
    theta,
    edge_weight,
    inner_edge,
    crossing_segment,
    cut_dest,
    crossing_hyperedge,
    cotangent,
):
    seg = feats.shape[0]
    n_region = lax.axis_size("region")
    n_sub = lax.axis_size("sub")
    device_list = n_region * n_sub
    slot_capacity = max(2, 2 * crossing_segment.shape[0] // device_list)
    slot_total = device_list * slot_capacity
    width = TP * B * C
    def front(rows):
        n = rows.shape[0]
        x4 = rows.reshape(n, T_SIZE, B, C)
        stack = jnp.concatenate([x4[:, k : k + TP] for k in range(KT)], axis=-1)
        u = (
            jnp.einsum("stbk,kf->stbf", stack, conv_weight, preferred_element_type=jnp.float32)
            + conv_bias
        )
        gate = jax.nn.sigmoid(u[..., C:])
        first = u[..., :C]
        hidden = (first * gate).astype(jnp.bfloat16)
        z = (
            jnp.einsum("stbc,cd->stbd", hidden, theta, preferred_element_type=jnp.float32)
            .astype(jnp.bfloat16)
            .reshape(n, width)
        )
        return stack, gate, first, hidden, z

    edge_index = jnp.arange(EDGE_DEV, dtype=jnp.int32)
    incidence = jnp.zeros((EDGE_DEV, seg), jnp.float32)
    for m in range(MEM):
        incidence = incidence + (inner_edge[:, m][None, :] == edge_index[:, None]).astype(
            jnp.float32
        )
    inner_count = jnp.sum(incidence, axis=1)
    incidence = incidence.astype(jnp.bfloat16)
    dest = cut_dest[:, 0]
    n_cut = dest.shape[0]
    order = jnp.arange(n_cut, dtype=jnp.int32)
    earlier = (dest[None, :] == dest[:, None]) & (order[None, :] < order[:, None])
    rank = jnp.sum(earlier.astype(jnp.int32), axis=1)
    slot_position = dest * slot_capacity + rank
    slot_hot = (slot_position[:, None] == jnp.arange(slot_total, dtype=jnp.int32)[None, :]).astype(
        jnp.int32
    )
    slotted_segment = jnp.sum(slot_hot * (crossing_segment[:, None] + 1), axis=0) - 1
    slotted_hyperedge = jnp.sum(slot_hot * (crossing_hyperedge[:, None] + 1), axis=0) - 1
    members = (slotted_segment[None, :] == jnp.arange(seg, dtype=jnp.int32)[:, None]).astype(
        jnp.float32
    )
    degree = (MEM + jnp.sum(members, axis=1))[:, None]
    members = members.astype(jnp.bfloat16)
    def pick_slots(rows):
        return jnp.einsum("sn,sf->nf", members, rows, preferred_element_type=jnp.float32).astype(
            jnp.bfloat16
        )

    cut_rows = pick_slots(feats)
    stack, gate, first, hidden, z = front(feats)

    edge_cols = jnp.broadcast_to(slotted_hyperedge.astype(jnp.bfloat16)[:, None], (slot_total, 128))
    in_width = feats.shape[1]
    send = jnp.concatenate([cut_rows, edge_cols], axis=1)
    recv_all = lax.all_to_all(send, ("region", "sub"), split_axis=0, concat_axis=0, tiled=True)
    r_stack, r_gate, r_first, r_hidden, recv = front(recv_all[:, :in_width])
    recv_edge = recv_all[:, in_width].astype(jnp.int32)
    owned = (recv_edge[None, :] == edge_index[:, None]).astype(jnp.float32)
    count = 1.0 + inner_count + jnp.sum(owned, axis=1)
    owned = owned.astype(jnp.bfloat16)
    scale = (edge_weight / count)[:, None]

    def edge_side(local_rows, arrived):
        total = jnp.dot(incidence, local_rows, preferred_element_type=jnp.float32) + jnp.dot(
            owned, arrived, preferred_element_type=jnp.float32
        )
        values = (scale * total).astype(jnp.bfloat16)
        returned = jnp.einsum(
            "en,ef->nf", owned, values, preferred_element_type=jnp.float32
        ).astype(jnp.bfloat16)
        return (values, returned)

    def member_side(values, back):
        return jnp.einsum(
            "es,ef->sf", incidence, values, preferred_element_type=jnp.float32
        ) + jnp.dot(members, back, preferred_element_type=jnp.float32)

    edge_val, ret_rows = edge_side(z, recv)
    back = lax.all_to_all(ret_rows, ("region", "sub"), split_axis=0, concat_axis=0, tiled=True)
    y = member_side(edge_val, back) / degree
    sig_y = jax.nn.sigmoid(y)
    block_out = (y * sig_y).astype(jnp.bfloat16)
    dy = cotangent.astype(jnp.float32) * sig_y * (1.0 + y * (1.0 - sig_y))
    grad_rows = (dy / degree).astype(jnp.bfloat16)
    send_grads = pick_slots(grad_rows)
    recv_grads = lax.all_to_all(
        send_grads, ("region", "sub"), split_axis=0, concat_axis=0, tiled=True
    )
    dedge, ret_grads = edge_side(grad_rows, recv_grads)
    inner_sum = jnp.einsum("es,ef->sf", incidence, dedge, preferred_element_type=jnp.float32)
    dz_slots = jnp.einsum(
        "en,etbd->ntbd", owned, dedge.reshape(EDGE_DEV, TP, B, C), preferred_element_type=jnp.float32
    ).astype(jnp.bfloat16)
    inner_sum, dz_slots, ret_grads = lax.optimization_barrier((inner_sum, dz_slots, ret_grads))
    back_grads = lax.all_to_all(
        ret_grads, ("region", "sub"), split_axis=0, concat_axis=0, tiled=True
    )

    def weight_grads(st, gt, fi, hi, dzr):
        g_theta = jnp.einsum("stbc,stbd->cd", hi, dzr, preferred_element_type=jnp.float32)
        dh = jnp.einsum("stbd,cd->stbc", dzr, theta, preferred_element_type=jnp.float32)
        du = jnp.concatenate([dh * gt, dh * fi * gt * (1.0 - gt)], axis=-1).astype(jnp.bfloat16)
        g_conv = jnp.einsum("stbk,stbf->kf", st, du, preferred_element_type=jnp.float32)
        g_bias = jnp.sum(du.astype(jnp.float32), axis=(0, 1, 2))
        return du, g_conv, g_bias, g_theta

    dz_inner = inner_sum.astype(jnp.bfloat16).reshape(seg, TP, B, C)
    _, ga_conv, ga_bias, ga_theta = weight_grads(stack, gate, first, hidden, dz_inner)
    _, gb_conv, gb_bias, gb_theta = weight_grads(r_stack, r_gate, r_first, r_hidden, dz_slots)
    partial = (ga_conv + gb_conv, ga_bias + gb_bias, ga_theta + gb_theta)
    (sum_conv, sum_bias, sum_theta), back_grads = device_sum(partial, device_list, back_grads)
    dz = (
        (inner_sum + jnp.dot(members, back_grads, preferred_element_type=jnp.float32))
        .astype(jnp.bfloat16)
        .reshape(seg, TP, B, C)
    )
    dh = jnp.einsum("stbd,cd->stbc", dz, theta, preferred_element_type=jnp.float32)
    du = jnp.concatenate([dh * gate, dh * first * gate * (1.0 - gate)], axis=-1).astype(
        jnp.bfloat16
    )
    norm = 1.0 / jnp.sqrt(jnp.float32(seg * device_list * TP * B))
    dstack = jnp.einsum("stbf,kf->stbk", du, conv_weight, preferred_element_type=jnp.float32)
    grad_sum = jnp.zeros((seg, T_SIZE, B, C), jnp.float32)
    for k in range(KT):
        grad_sum = grad_sum + jnp.pad(
            dstack[..., k * C : (k + 1) * C], ((0, 0), (k, KT - 1 - k), (0, 0), (0, 0))
        )
    grad_feats = grad_sum.astype(jnp.bfloat16).reshape(seg, T_SIZE * B * C)
    return (block_out, grad_feats, sum_conv * norm, sum_bias * norm, sum_theta * norm)


def solution(mesh):
    in_specs = (
        P(("region", "sub"), None),
        P(),
        P(),
        P(),
        P(("region", "sub")),
        P(("region", "sub"), None),
        P(("region", "sub")),
        P(("region", "sub"), None),
        P(("region", "sub")),
        P(("region", "sub"), None),
    )
    out_specs = (P(("region", "sub"), None), P(("region", "sub"), None), P(), P(), P())
    return jax.shard_map(body, mesh=mesh, in_specs=in_specs, out_specs=out_specs, check_vma=False)
```

```python
import jax
import jax.numpy as jnp
from jax import lax
from jax.sharding import PartitionSpec as P

C = 64
T_SIZE = 12
B = 2
KT = 3
MEM = 2
TP = 10
EDGE_DEV = 128


def device_sum(parts, n):
    sizes = [p.size for p in parts]
    flat = jnp.concatenate([p.reshape(-1) for p in parts])
    if n & (n - 1):
        flat = lax.psum(flat, ("region", "sub"))
    else:
        step = 1
        while step < n:
            perm = [(i, i ^ step) for i in range(n)]
            flat = flat + lax.ppermute(flat, ("region", "sub"), perm)
            step *= 2
    out, at = [], 0
    for p, size in zip(parts, sizes):
        out.append(flat[at : at + size].reshape(p.shape))
        at += size
    return out


def body(
    feats,
    conv_weight,
    conv_bias,
    theta,
    edge_weight,
    inner_edge,
    crossing_segment,
    cut_dest,
    crossing_hyperedge,
    cotangent,
):
    seg = feats.shape[0]
    n_region = lax.axis_size("region")
    n_sub = lax.axis_size("sub")
    device_list = n_region * n_sub
    slot_capacity = max(2, 2 * crossing_segment.shape[0] // device_list)
    slot_total = device_list * slot_capacity
    width = TP * B * C
    def front(rows):
        n = rows.shape[0]
        x4 = rows.reshape(n, T_SIZE, B, C)
        stack = jnp.concatenate([x4[:, k : k + TP] for k in range(KT)], axis=-1)
        u = (
            jnp.einsum("stbk,kf->stbf", stack, conv_weight, preferred_element_type=jnp.float32)
            + conv_bias
        )
        gate = jax.nn.sigmoid(u[..., C:])
        first = u[..., :C]
        hidden = (first * gate).astype(jnp.bfloat16)
        z = (
            jnp.einsum("stbc,cd->stbd", hidden, theta, preferred_element_type=jnp.float32)
            .astype(jnp.bfloat16)
            .reshape(n, width)
        )
        return stack, gate, first, hidden, z

    edge_index = jnp.arange(EDGE_DEV, dtype=jnp.int32)
    incidence = jnp.zeros((EDGE_DEV, seg), jnp.float32)
    for m in range(MEM):
        incidence = incidence + (inner_edge[:, m][None, :] == edge_index[:, None]).astype(
            jnp.float32
        )
    inner_count = jnp.sum(incidence, axis=1)
    incidence = incidence.astype(jnp.bfloat16)
    dest = cut_dest[:, 0]
    n_cut = dest.shape[0]
    order = jnp.arange(n_cut, dtype=jnp.int32)
    earlier = (dest[None, :] == dest[:, None]) & (order[None, :] < order[:, None])
    rank = jnp.sum(earlier.astype(jnp.int32), axis=1)
    slot_position = dest * slot_capacity + rank
    slot_hot = (slot_position[:, None] == jnp.arange(slot_total, dtype=jnp.int32)[None, :]).astype(
        jnp.int32
    )
    slotted_segment = jnp.sum(slot_hot * (crossing_segment[:, None] + 1), axis=0) - 1
    slotted_hyperedge = jnp.sum(slot_hot * (crossing_hyperedge[:, None] + 1), axis=0) - 1
    members = (slotted_segment[None, :] == jnp.arange(seg, dtype=jnp.int32)[:, None]).astype(
        jnp.float32
    )
    degree = (MEM + jnp.sum(members, axis=1))[:, None]
    members = members.astype(jnp.bfloat16)
    def pick_slots(rows):
        return jnp.einsum("sn,sf->nf", members, rows, preferred_element_type=jnp.float32).astype(
            jnp.bfloat16
        )

    cut_rows = pick_slots(feats)
    stack, gate, first, hidden, z = front(feats)

    edge_cols = jnp.broadcast_to(slotted_hyperedge.astype(jnp.bfloat16)[:, None], (slot_total, 128))
    in_width = feats.shape[1]
    send = jnp.concatenate([cut_rows, edge_cols], axis=1)
    recv_all = lax.all_to_all(send, ("region", "sub"), split_axis=0, concat_axis=0, tiled=True)
    r_stack, r_gate, r_first, r_hidden, recv = front(recv_all[:, :in_width])
    recv_edge = recv_all[:, in_width].astype(jnp.int32)
    owned = (recv_edge[None, :] == edge_index[:, None]).astype(jnp.float32)
    count = 1.0 + inner_count + jnp.sum(owned, axis=1)
    owned = owned.astype(jnp.bfloat16)
    scale = (edge_weight / count)[:, None]

    def edge_side(local_rows, arrived):
        total = jnp.dot(incidence, local_rows, preferred_element_type=jnp.float32) + jnp.dot(
            owned, arrived, preferred_element_type=jnp.float32
        )
        values = (scale * total).astype(jnp.bfloat16)
        returned = jnp.einsum(
            "en,ef->nf", owned, values, preferred_element_type=jnp.float32
        ).astype(jnp.bfloat16)
        return (values, returned)

    def member_side(values, back):
        return jnp.einsum(
            "es,ef->sf", incidence, values, preferred_element_type=jnp.float32
        ) + jnp.dot(members, back, preferred_element_type=jnp.float32)

    edge_val, ret_rows = edge_side(z, recv)
    back = lax.all_to_all(ret_rows, ("region", "sub"), split_axis=0, concat_axis=0, tiled=True)
    y = member_side(edge_val, back) / degree
    sig_y = jax.nn.sigmoid(y)
    dy = cotangent.astype(jnp.float32) * sig_y * (1.0 + y * (1.0 - sig_y))
    grad_rows = (dy / degree).astype(jnp.bfloat16)
    send_grads = pick_slots(grad_rows)
    recv_grads = lax.all_to_all(
        send_grads, ("region", "sub"), split_axis=0, concat_axis=0, tiled=True
    )
    dedge, ret_grads = edge_side(grad_rows, recv_grads)
    inner_sum = jnp.einsum("es,ef->sf", incidence, dedge, preferred_element_type=jnp.float32)
    dz_slots = jnp.einsum(
        "en,etbd->ntbd", owned, dedge.reshape(EDGE_DEV, TP, B, C), preferred_element_type=jnp.float32
    ).astype(jnp.bfloat16)
    inner_sum, dz_slots, ret_grads = lax.optimization_barrier((inner_sum, dz_slots, ret_grads))
    back_grads = lax.all_to_all(
        ret_grads, ("region", "sub"), split_axis=0, concat_axis=0, tiled=True
    )

    def weight_grads(st, gt, fi, hi, dzr):
        g_theta = jnp.einsum("stbc,stbd->cd", hi, dzr, preferred_element_type=jnp.float32)
        dh = jnp.einsum("stbd,cd->stbc", dzr, theta, preferred_element_type=jnp.float32)
        du = jnp.concatenate([dh * gt, dh * fi * gt * (1.0 - gt)], axis=-1).astype(jnp.bfloat16)
        g_conv = jnp.einsum("stbk,stbf->kf", st, du, preferred_element_type=jnp.float32)
        g_bias = jnp.sum(du.astype(jnp.float32), axis=(0, 1, 2))
        return du, g_conv, g_bias, g_theta

    dz_inner = inner_sum.astype(jnp.bfloat16).reshape(seg, TP, B, C)
    _, ga_conv, ga_bias, ga_theta = weight_grads(stack, gate, first, hidden, dz_inner)
    _, gb_conv, gb_bias, gb_theta = weight_grads(r_stack, r_gate, r_first, r_hidden, dz_slots)
    partial = (ga_conv + gb_conv, ga_bias + gb_bias, ga_theta + gb_theta)
    partial, back_grads, late_val, late_back = lax.optimization_barrier(
        (partial, back_grads, edge_val, back)
    )
    y_late = member_side(late_val, late_back) / degree
    block_out = (y_late * jax.nn.sigmoid(y_late)).astype(jnp.bfloat16)
    sum_conv, sum_bias, sum_theta = device_sum(partial, device_list)
    dz = (
        (inner_sum + jnp.dot(members, back_grads, preferred_element_type=jnp.float32))
        .astype(jnp.bfloat16)
        .reshape(seg, TP, B, C)
    )
    dh = jnp.einsum("stbd,cd->stbc", dz, theta, preferred_element_type=jnp.float32)
    du = jnp.concatenate([dh * gate, dh * first * gate * (1.0 - gate)], axis=-1).astype(
        jnp.bfloat16
    )
    norm = 1.0 / jnp.sqrt(jnp.float32(seg * device_list * TP * B))
    dstack = jnp.einsum("stbf,kf->stbk", du, conv_weight, preferred_element_type=jnp.float32)
    grad_sum = jnp.zeros((seg, T_SIZE, B, C), jnp.float32)
    for k in range(KT):
        grad_sum = grad_sum + jnp.pad(
            dstack[..., k * C : (k + 1) * C], ((0, 0), (k, KT - 1 - k), (0, 0), (0, 0))
        )
    grad_feats = grad_sum.astype(jnp.bfloat16).reshape(seg, T_SIZE * B * C)
    return (block_out, grad_feats, sum_conv * norm, sum_bias * norm, sum_theta * norm)


def solution(mesh):
    in_specs = (
        P(("region", "sub"), None),
        P(),
        P(),
        P(),
        P(("region", "sub")),
        P(("region", "sub"), None),
        P(("region", "sub")),
        P(("region", "sub"), None),
        P(("region", "sub")),
        P(("region", "sub"), None),
    )
    out_specs = (P(("region", "sub"), None), P(("region", "sub"), None), P(), P(), P())
    return jax.shard_map(body, mesh=mesh, in_specs=in_specs, out_specs=out_specs, check_vma=False)
```

```python
import jax
import jax.numpy as jnp
from jax import lax
from jax.sharding import PartitionSpec as P

C = 64
T_SIZE = 12
B = 2
KT = 3
MEM = 2
TP = 10
EDGE_DEV = 128


def device_sum(parts, n):
    sizes = [p.size for p in parts]
    flat = jnp.concatenate([p.reshape(-1) for p in parts])
    if n & (n - 1):
        flat = lax.psum(flat, ("region", "sub"))
    else:
        step = 1
        while step < n:
            perm = [(i, i ^ step) for i in range(n)]
            flat = flat + lax.ppermute(flat, ("region", "sub"), perm)
            step *= 2
    out, at = [], 0
    for p, size in zip(parts, sizes):
        out.append(flat[at : at + size].reshape(p.shape))
        at += size
    return out


def body(
    feats,
    conv_weight,
    conv_bias,
    theta,
    edge_weight,
    inner_edge,
    crossing_segment,
    cut_dest,
    crossing_hyperedge,
    cotangent,
):
    seg = feats.shape[0]
    n_region = lax.axis_size("region")
    n_sub = lax.axis_size("sub")
    device_list = n_region * n_sub
    slot_capacity = max(2, 2 * crossing_segment.shape[0] // device_list)
    slot_total = device_list * slot_capacity
    width = TP * B * C
    def front(rows):
        n = rows.shape[0]
        x4 = rows.reshape(n, T_SIZE, B, C)
        stack = jnp.concatenate([x4[:, k : k + TP] for k in range(KT)], axis=-1)
        u = (
            jnp.einsum("stbk,kf->stbf", stack, conv_weight, preferred_element_type=jnp.float32)
            + conv_bias
        )
        gate = jax.nn.sigmoid(u[..., C:])
        first = u[..., :C]
        hidden = (first * gate).astype(jnp.bfloat16)
        z = (
            jnp.einsum("stbc,cd->stbd", hidden, theta, preferred_element_type=jnp.float32)
            .astype(jnp.bfloat16)
            .reshape(n, width)
        )
        return stack, gate, first, hidden, z

    edge_index = jnp.arange(EDGE_DEV, dtype=jnp.int32)
    incidence = jnp.zeros((EDGE_DEV, seg), jnp.float32)
    for m in range(MEM):
        incidence = incidence + (inner_edge[:, m][None, :] == edge_index[:, None]).astype(
            jnp.float32
        )
    inner_count = jnp.sum(incidence, axis=1)
    incidence = incidence.astype(jnp.bfloat16)
    dest = cut_dest[:, 0]
    n_cut = dest.shape[0]
    order = jnp.arange(n_cut, dtype=jnp.int32)
    earlier = (dest[None, :] == dest[:, None]) & (order[None, :] < order[:, None])
    rank = jnp.sum(earlier.astype(jnp.int32), axis=1)
    slot_position = dest * slot_capacity + rank
    slot_hot = (slot_position[:, None] == jnp.arange(slot_total, dtype=jnp.int32)[None, :]).astype(
        jnp.int32
    )
    slotted_segment = jnp.sum(slot_hot * (crossing_segment[:, None] + 1), axis=0) - 1
    slotted_hyperedge = jnp.sum(slot_hot * (crossing_hyperedge[:, None] + 1), axis=0) - 1
    members = (slotted_segment[None, :] == jnp.arange(seg, dtype=jnp.int32)[:, None]).astype(
        jnp.float32
    )
    degree = (MEM + jnp.sum(members, axis=1))[:, None]
    members = members.astype(jnp.bfloat16)
    def pick_slots(rows):
        return jnp.einsum("sn,sf->nf", members, rows, preferred_element_type=jnp.float32).astype(
            jnp.bfloat16
        )

    cut_rows = pick_slots(feats)
    stack, gate, first, hidden, z = front(feats)

    edge_cols = jnp.broadcast_to(slotted_hyperedge.astype(jnp.bfloat16)[:, None], (slot_total, 128))
    in_width = feats.shape[1]
    send = jnp.concatenate([cut_rows, edge_cols], axis=1)
    recv_all = lax.all_to_all(send, ("region", "sub"), split_axis=0, concat_axis=0, tiled=True)
    r_stack, r_gate, r_first, r_hidden, recv = front(recv_all[:, :in_width])
    recv_edge = recv_all[:, in_width].astype(jnp.int32)
    owned = (recv_edge[None, :] == edge_index[:, None]).astype(jnp.float32)
    count = 1.0 + inner_count + jnp.sum(owned, axis=1)
    owned = owned.astype(jnp.bfloat16)
    scale = (edge_weight / count)[:, None]

    def edge_side(local_rows, arrived):
        total = jnp.dot(incidence, local_rows, preferred_element_type=jnp.float32) + jnp.dot(
            owned, arrived, preferred_element_type=jnp.float32
        )
        values = (scale * total).astype(jnp.bfloat16)
        returned = jnp.einsum(
            "en,ef->nf", owned, values, preferred_element_type=jnp.float32
        ).astype(jnp.bfloat16)
        return (values, returned)

    def member_side(values, back):
        return jnp.einsum(
            "es,ef->sf", incidence, values, preferred_element_type=jnp.float32
        ) + jnp.dot(members, back, preferred_element_type=jnp.float32)

    edge_val, ret_rows = edge_side(z, recv)
    back = lax.all_to_all(ret_rows, ("region", "sub"), split_axis=0, concat_axis=0, tiled=True)
    y = member_side(edge_val, back) / degree
    sig_y = jax.nn.sigmoid(y)
    block_out = (y * sig_y).astype(jnp.bfloat16)
    dy = cotangent.astype(jnp.float32) * sig_y * (1.0 + y * (1.0 - sig_y))
    grad_rows = (dy / degree).astype(jnp.bfloat16)
    send_grads = pick_slots(grad_rows)
    recv_grads = lax.all_to_all(
        send_grads, ("region", "sub"), split_axis=0, concat_axis=0, tiled=True
    )
    dedge, ret_grads = edge_side(grad_rows, recv_grads)
    inner_sum = jnp.einsum("es,ef->sf", incidence, dedge, preferred_element_type=jnp.float32)
    dz_slots = jnp.einsum(
        "en,etbd->ntbd", owned, dedge.reshape(EDGE_DEV, TP, B, C), preferred_element_type=jnp.float32
    ).astype(jnp.bfloat16)
    inner_sum, dz_slots, ret_grads = lax.optimization_barrier((inner_sum, dz_slots, ret_grads))
    back_grads = lax.all_to_all(
        ret_grads, ("region", "sub"), split_axis=0, concat_axis=0, tiled=True
    )

    def weight_grads(st, gt, fi, hi, dzr):
        g_theta = jnp.einsum("stbc,stbd->cd", hi, dzr, preferred_element_type=jnp.float32)
        dh = jnp.einsum("stbd,cd->stbc", dzr, theta, preferred_element_type=jnp.float32)
        du = jnp.concatenate([dh * gt, dh * fi * gt * (1.0 - gt)], axis=-1).astype(jnp.bfloat16)
        g_conv = jnp.einsum("stbk,stbf->kf", st, du, preferred_element_type=jnp.float32)
        g_bias = jnp.sum(du.astype(jnp.float32), axis=(0, 1, 2))
        return du, g_conv, g_bias, g_theta

    dz_inner = inner_sum.astype(jnp.bfloat16).reshape(seg, TP, B, C)
    _, ga_conv, ga_bias, ga_theta = weight_grads(stack, gate, first, hidden, dz_inner)
    _, gb_conv, gb_bias, gb_theta = weight_grads(r_stack, r_gate, r_first, r_hidden, dz_slots)
    norm = 1.0 / jnp.sqrt(jnp.float32(seg * device_list * TP * B))
    partial = ((ga_conv + gb_conv) * norm, (ga_bias + gb_bias) * norm, (ga_theta + gb_theta) * norm)
    partial, back_grads = lax.optimization_barrier((partial, back_grads))
    sum_conv, sum_bias, sum_theta = device_sum(partial, device_list)
    dz = (
        (inner_sum + jnp.dot(members, back_grads, preferred_element_type=jnp.float32))
        .astype(jnp.bfloat16)
        .reshape(seg, TP, B, C)
    )
    dh = jnp.einsum("stbd,cd->stbc", dz, theta, preferred_element_type=jnp.float32)
    du = jnp.concatenate([dh * gate, dh * first * gate * (1.0 - gate)], axis=-1).astype(
        jnp.bfloat16
    )
    dstack = jnp.einsum("stbf,kf->stbk", du, conv_weight, preferred_element_type=jnp.float32)
    grad_sum = jnp.zeros((seg, T_SIZE, B, C), jnp.float32)
    for k in range(KT):
        grad_sum = grad_sum + jnp.pad(
            dstack[..., k * C : (k + 1) * C], ((0, 0), (k, KT - 1 - k), (0, 0), (0, 0))
        )
    grad_feats = grad_sum.astype(jnp.bfloat16).reshape(seg, T_SIZE * B * C)
    return (block_out, grad_feats, sum_conv, sum_bias, sum_theta)


def solution(mesh):
    in_specs = (
        P(("region", "sub"), None),
        P(),
        P(),
        P(),
        P(("region", "sub")),
        P(("region", "sub"), None),
        P(("region", "sub")),
        P(("region", "sub"), None),
        P(("region", "sub")),
        P(("region", "sub"), None),
    )
    out_specs = (P(("region", "sub"), None), P(("region", "sub"), None), P(), P(), P())
    return jax.shard_map(body, mesh=mesh, in_specs=in_specs, out_specs=out_specs, check_vma=False)
```

```python
import jax
import jax.numpy as jnp
from jax import lax
from jax.sharding import PartitionSpec as P

C = 64
T_SIZE = 12
B = 2
KT = 3
MEM = 2
TP = 10
EDGE_DEV = 128


def device_sum(parts, n, tie):
    sizes = [p.size for p in parts]
    flat = jnp.concatenate([p.reshape(-1) for p in parts])
    if n & (n - 1):
        flat, tie = lax.optimization_barrier((flat, tie))
        flat = lax.psum(flat, ("region", "sub"))
    else:
        step = 1
        while step < n:
            perm = [(i, i ^ step) for i in range(n)]
            flat = flat + lax.ppermute(flat, ("region", "sub"), perm)
            if step == 1:
                flat, tie = lax.optimization_barrier((flat, tie))
            step *= 2
        if n == 1:
            flat, tie = lax.optimization_barrier((flat, tie))
    out, at = [], 0
    for p, size in zip(parts, sizes):
        out.append(flat[at : at + size].reshape(p.shape))
        at += size
    return out, tie


def body(
    feats,
    conv_weight,
    conv_bias,
    theta,
    edge_weight,
    inner_edge,
    crossing_segment,
    cut_dest,
    crossing_hyperedge,
    cotangent,
):
    seg = feats.shape[0]
    n_region = lax.axis_size("region")
    n_sub = lax.axis_size("sub")
    device_list = n_region * n_sub
    slot_capacity = max(2, 2 * crossing_segment.shape[0] // device_list)
    slot_total = device_list * slot_capacity
    width = TP * B * C
    def front(rows):
        n = rows.shape[0]
        x4 = rows.reshape(n, T_SIZE, B, C)
        stack = jnp.concatenate([x4[:, k : k + TP] for k in range(KT)], axis=-1)
        u = (
            jnp.einsum("stbk,kf->stbf", stack, conv_weight, preferred_element_type=jnp.float32)
            + conv_bias
        )
        gate = jax.nn.sigmoid(u[..., C:])
        first = u[..., :C]
        hidden = (first * gate).astype(jnp.bfloat16)
        z = (
            jnp.einsum("stbc,cd->stbd", hidden, theta, preferred_element_type=jnp.float32)
            .astype(jnp.bfloat16)
            .reshape(n, width)
        )
        return stack, gate, first, hidden, z

    edge_index = jnp.arange(EDGE_DEV, dtype=jnp.int32)
    incidence = jnp.zeros((EDGE_DEV, seg), jnp.float32)
    for m in range(MEM):
        incidence = incidence + (inner_edge[:, m][None, :] == edge_index[:, None]).astype(
            jnp.float32
        )
    inner_count = jnp.sum(incidence, axis=1)
    incidence = incidence.astype(jnp.bfloat16)
    dest = cut_dest[:, 0]
    n_cut = dest.shape[0]
    order = jnp.arange(n_cut, dtype=jnp.int32)
    earlier = (dest[None, :] == dest[:, None]) & (order[None, :] < order[:, None])
    rank = jnp.sum(earlier.astype(jnp.int32), axis=1)
    slot_position = dest * slot_capacity + rank
    slot_hot = (slot_position[:, None] == jnp.arange(slot_total, dtype=jnp.int32)[None, :]).astype(
        jnp.int32
    )
    slotted_segment = jnp.sum(slot_hot * (crossing_segment[:, None] + 1), axis=0) - 1
    slotted_hyperedge = jnp.sum(slot_hot * (crossing_hyperedge[:, None] + 1), axis=0) - 1
    members = (slotted_segment[None, :] == jnp.arange(seg, dtype=jnp.int32)[:, None]).astype(
        jnp.float32
    )
    degree = (MEM + jnp.sum(members, axis=1))[:, None]
    members = members.astype(jnp.bfloat16)
    def pick_slots(rows):
        return jnp.einsum("sn,sf->nf", members, rows, preferred_element_type=jnp.float32).astype(
            jnp.bfloat16
        )

    cut_rows = pick_slots(feats)
    stack, gate, first, hidden, z = front(feats)

    edge_cols = jnp.broadcast_to(slotted_hyperedge.astype(jnp.bfloat16)[:, None], (slot_total, 128))
    in_width = feats.shape[1]
    send = jnp.concatenate([cut_rows, edge_cols], axis=1)
    recv_all = lax.all_to_all(send, ("region", "sub"), split_axis=0, concat_axis=0, tiled=True)
    r_stack, r_gate, r_first, r_hidden, recv = front(recv_all[:, :in_width])
    recv_edge = recv_all[:, in_width].astype(jnp.int32)
    owned = (recv_edge[None, :] == edge_index[:, None]).astype(jnp.float32)
    count = 1.0 + inner_count + jnp.sum(owned, axis=1)
    owned = owned.astype(jnp.bfloat16)
    scale = (edge_weight / count)[:, None]

    def edge_side(local_rows, arrived):
        total = jnp.dot(incidence, local_rows, preferred_element_type=jnp.float32) + jnp.dot(
            owned, arrived, preferred_element_type=jnp.float32
        )
        values = (scale * total).astype(jnp.bfloat16)
        returned = jnp.einsum(
            "en,ef->nf", owned, values, preferred_element_type=jnp.float32
        ).astype(jnp.bfloat16)
        return (values, returned)

    def member_side(values, back):
        return jnp.einsum(
            "es,ef->sf", incidence, values, preferred_element_type=jnp.float32
        ) + jnp.dot(members, back, preferred_element_type=jnp.float32)

    edge_val, ret_rows = edge_side(z, recv)
    back = lax.all_to_all(ret_rows, ("region", "sub"), split_axis=0, concat_axis=0, tiled=True)
    y = member_side(edge_val, back) / degree
    sig_y = jax.nn.sigmoid(y)
    block_out = (y * sig_y).astype(jnp.bfloat16)
    dy = cotangent.astype(jnp.float32) * sig_y * (1.0 + y * (1.0 - sig_y))
    grad_rows = (dy / degree).astype(jnp.bfloat16)
    send_grads = pick_slots(grad_rows)
    recv_grads = lax.all_to_all(
        send_grads, ("region", "sub"), split_axis=0, concat_axis=0, tiled=True
    )
    dedge, ret_grads = edge_side(grad_rows, recv_grads)
    inner_sum = jnp.einsum("es,ef->sf", incidence, dedge, preferred_element_type=jnp.float32)
    dz_slots = jnp.einsum(
        "en,etbd->ntbd", owned, dedge.reshape(EDGE_DEV, TP, B, C), preferred_element_type=jnp.float32
    ).astype(jnp.bfloat16)
    inner_sum, dz_slots, ret_grads = lax.optimization_barrier((inner_sum, dz_slots, ret_grads))
    back_grads = lax.all_to_all(
        ret_grads, ("region", "sub"), split_axis=0, concat_axis=0, tiled=True
    )

    def weight_grads(st, gt, fi, hi, dzr):
        g_theta = jnp.einsum("stbc,stbd->cd", hi, dzr, preferred_element_type=jnp.float32)
        dh = jnp.einsum("stbd,cd->stbc", dzr, theta, preferred_element_type=jnp.float32)
        du = jnp.concatenate([dh * gt, dh * fi * gt * (1.0 - gt)], axis=-1).astype(jnp.bfloat16)
        g_conv = jnp.einsum("stbk,stbf->kf", st, du, preferred_element_type=jnp.float32)
        g_bias = jnp.sum(du.astype(jnp.float32), axis=(0, 1, 2))
        return du, g_conv, g_bias, g_theta

    dz_inner = inner_sum.astype(jnp.bfloat16).reshape(seg, TP, B, C)
    _, ga_conv, ga_bias, ga_theta = weight_grads(stack, gate, first, hidden, dz_inner)
    _, gb_conv, gb_bias, gb_theta = weight_grads(r_stack, r_gate, r_first, r_hidden, dz_slots)
    norm = 1.0 / jnp.sqrt(jnp.float32(seg * device_list * TP * B))
    partial = ((ga_conv + gb_conv) * norm, (ga_bias + gb_bias) * norm, (ga_theta + gb_theta) * norm)
    (sum_conv, sum_bias, sum_theta), back_grads = device_sum(partial, device_list, back_grads)
    dz = (
        (inner_sum + jnp.dot(members, back_grads, preferred_element_type=jnp.float32))
        .astype(jnp.bfloat16)
        .reshape(seg, TP, B, C)
    )
    dh = jnp.einsum("stbd,cd->stbc", dz, theta, preferred_element_type=jnp.float32)
    du = jnp.concatenate([dh * gate, dh * first * gate * (1.0 - gate)], axis=-1).astype(
        jnp.bfloat16
    )
    dstack = jnp.einsum("stbf,kf->stbk", du, conv_weight, preferred_element_type=jnp.float32)
    grad_sum = jnp.zeros((seg, T_SIZE, B, C), jnp.float32)
    for k in range(KT):
        grad_sum = grad_sum + jnp.pad(
            dstack[..., k * C : (k + 1) * C], ((0, 0), (k, KT - 1 - k), (0, 0), (0, 0))
        )
    grad_feats = grad_sum.astype(jnp.bfloat16).reshape(seg, T_SIZE * B * C)
    return (block_out, grad_feats, sum_conv, sum_bias, sum_theta)


def solution(mesh):
    in_specs = (
        P(("region", "sub"), None),
        P(),
        P(),
        P(),
        P(("region", "sub")),
        P(("region", "sub"), None),
        P(("region", "sub")),
        P(("region", "sub"), None),
        P(("region", "sub")),
        P(("region", "sub"), None),
    )
    out_specs = (P(("region", "sub"), None), P(("region", "sub"), None), P(), P(), P())
    return jax.shard_map(body, mesh=mesh, in_specs=in_specs, out_specs=out_specs, check_vma=False)
```
